32 devices in a mesh: expert: 4 (over y, x), dp: 8 (over z, core).
Axes of the slice: x: 2, y: 2, z: 4, core: 2. Of those that a mesh axis runs over, the one named last changes fastest.
Arguments:
- out_grad: bfloat16 [4096, 2048], P(('expert', 'dp')), may hold values from -6 to 6
- combine_weight: float32 [4096, 2], P(('expert', 'dp')), may hold values from 0.02 to 0.5
- routes: int32 [4096, 2], P(('expert', 'dp')), may hold values from 0 to 3, all different within a row; in each aligned block of 128 rows (0 to 127, 128 to 255, ...) at most 96 rows name the same one
- saved_gate: bfloat16 [4, 8, 4, 96, 768], P('expert', 'dp'), may hold values from -6 to 6
- saved_up: bfloat16 [4, 8, 4, 96, 768], P('expert', 'dp'), may hold values from -6 to 6
- w_down: bfloat16 [4, 768, 2048], P('expert'), may hold values from -0.21875 to 0.21875
Outputs:
- grad_w_down: float32 [4, 768, 2048], P('expert', 'dp')
- grad_gate: bfloat16 [4, 8, 4, 96, 768], P('expert', 'dp')
- grad_up: bfloat16 [4, 8, 4, 96, 768], P('expert', 'dp')
- grad_combine: float32 [4096, 2], P(('expert', 'dp'))
The draws below stay inside these ranges and needn't reach their ends.
Inputs may be any that keep to these rules, and one draw needn't show every extreme that they name: The routes of a token name different experts. In the rows of one device (aligned blocks of 128 tokens) no expert is named by more than 96 routes, and every expert is named somewhere.
All inputs are finite; a program needn't handle non-finite values.
Results may differ from the reference program's by a relative error of at most 0.015.
Values may be sent and summed in bfloat16 or wider, within the bound.
No kernel may reach another device: no remote copies, remote signals or barrier semaphores. Data moves between devices by JAX's collectives and lax.ppermute only.
A program may use at most 64 MiB of HBM per device.

```python
import math
import jax
import jax.numpy as jnp
import numpy as np
from jax import lax

DW = 2048
HID = 768
ROUTES = 2
TOK_DEV = 128
EXPERTS = 4
CAP = 96
TOKENS = 4096
N_DP = 8


def strengthened(entries, stream_key, source, target, blocks, factor):
    def block_of(dim):
        return (jnp.arange(entries.shape[dim]) // (entries.shape[dim] // blocks)).reshape((-1,) + (1,) * (entries.ndim - 1 - dim))

    near = jax.random.permutation(stream_key, blocks)[block_of(target)]
    far = (block_of(target) + blocks // 2) % blocks
    return jnp.where((block_of(source) == near) | (block_of(source) == far), factor * entries, entries)


def block_scale(rng, dims, pieces, low, top_value):
    level = 1.0
    for axis_at, blocks in pieces:
        steps = jax.random.uniform(jax.random.fold_in(jax.random.fold_in(rng, 6), axis_at), (blocks,), jnp.float32, low / len(pieces), top_value / len(pieces))
        level = level * jnp.repeat(jnp.exp(steps), dims[axis_at] // blocks).reshape((-1,) + (1,) * (len(dims) - 1 - axis_at))
    return level


def routed_block(rng, own, number, rows, number_of, top, limit, slope):
    sequence = jax.random.permutation(rng, number_of)
    heavy_load, ordinary = load_shares(number_of, rows * top, limit, slope, True), load_shares(number_of, rows * top, limit, slope, False)
    places = jnp.arange(number_of)

    def named(lengths, rotation):
        used = int((lengths > 0).sum())
        fixed = max(1, used // 4)
        moved = fixed + (places - fixed + rotation * (used - fixed)) % max(1, number_of - fixed)
        return jnp.zeros((number_of,), jnp.int32).at[sequence[jnp.where(places < fixed, places, moved)]].set(jnp.asarray(lengths, jnp.int32))

    lengths = jnp.where(number % 4 == 0, named(heavy_load, number // 4), named(ordinary, number - number // 4 - 1))
    mixed = jax.random.permutation(jax.random.fold_in(own, 3), number_of)
    source_of, taker = mixed[0:number_of // 2 * 2:2], mixed[1:number_of // 2 * 2:2]
    room = jnp.minimum(lengths[source_of] - 1, limit - lengths[taker]) // 2
    room = jnp.where((source_of == sequence[0]) | (taker == sequence[0]) | (lengths[taker] == 0), 0, jnp.maximum(room, 0))
    moved = jax.random.randint(jax.random.fold_in(own, 4), (number_of // 2,), 0, 1 << 20) % (room + 1)
    lengths = lengths.at[source_of].add(-moved).at[taker].add(moved)
    labels = jnp.searchsorted(jnp.cumsum(lengths), jnp.arange(rows * top), side="right").astype(jnp.int32)
    listing = labels.reshape(top, rows).T
    listing = listing[jax.random.permutation(jax.random.fold_in(own, 1), rows)]
    rotation = jax.random.randint(jax.random.fold_in(own, 2), (rows, 1), 0, top)
    return jnp.take_along_axis(listing, (jnp.arange(top)[None, :] + rotation) % top, axis=1)


def load_shares(number_of, total, bound, skew, full):
    loads = [(1 << 20) // math.isqrt(grade ** skew) + 1 for grade in range(1, number_of + 1)]
    largest = bound if full else min(bound, max(-(-total // number_of), total * loads[0] // sum(loads)))
    least = 1 if total - largest >= number_of - 1 else 0
    given, surplus = [largest] + [least] * (number_of - 1), total - largest - least * (number_of - 1)
    while surplus > 0:
        free = [i for i in range(1, number_of) if given[i] < largest] or [i for i in range(1, number_of) if given[i] < bound]
        mass, remaining = sum([loads[i] for i in free]), surplus
        for i in free:
            addition = min(bound - given[i], max(1, remaining * loads[i] // mass), surplus)
            given[i] = given[i] + addition
            surplus = surplus - addition
    return np.array(given)


def scatter_about(stream_key, extent, width, most, pieces=(), kind=jnp.bfloat16):
    loudness = block_scale(stream_key, extent, pieces, -0.22, 0.18) if pieces else 1.0
    entries = jax.random.normal(stream_key, extent, jnp.float32) * width * loudness
    return jnp.minimum(jnp.maximum(entries, -most), most).astype(kind)


def heavy_noise(key, extent, deviation, limit, pieces, heavy, held_as=jnp.bfloat16):
    values = deviation * jax.random.normal(key, extent, jnp.float32)
    if pieces:
        values = values * block_scale(key, extent, pieces, -0.22, 0.18)
    return jnp.clip(strengthened(values, jax.random.fold_in(key, 3), *heavy), -limit, limit).astype(held_as)


def setup_inputs(seed: int = 0) -> dict:
    seeds = jax.random.split(jax.random.key(seed), 7)
    out_grad = scatter_about(seeds[0], (TOKENS, DW), 1.0, 6.0, ((0, 32),))
    combine_weight = jnp.clip(jnp.exp(math.log(0.5) - 3.218876 * jax.random.uniform(seeds[1], (TOKENS, ROUTES), jnp.float32) ** block_scale(seeds[1], (TOKENS, ROUTES), ((0, 32),), -0.2, 0.2)), 0.02, 0.5)
    routes_keys = jax.random.split(jax.random.fold_in(seeds[2], 1), TOKENS // TOK_DEV)
    routes_turns = jax.random.permutation(jax.random.fold_in(seeds[2], 3), TOKENS // TOK_DEV)
    routes = jax.vmap(lambda own, number: routed_block(jax.random.fold_in(seeds[2], 2), own, number, TOK_DEV, EXPERTS, ROUTES, CAP, 2))(routes_keys, routes_turns).reshape((TOKENS, ROUTES))
    saved_gate = scatter_about(seeds[3], (EXPERTS, N_DP, EXPERTS, CAP, HID), 1.0, 6.0, ((0, 4), (1, 8)))
    saved_up = heavy_noise(seeds[4], (EXPERTS, N_DP, EXPERTS, CAP, HID), 1.0, 6.0, ((0, 4), (1, 8)), (1, 4, 8, 2.0))
    w_down = scatter_about(seeds[5], (EXPERTS, HID, DW), HID ** -0.5, 0.21875, ((0, 4),))
    return dict(out_grad=out_grad, combine_weight=combine_weight, routes=routes, saved_gate=saved_gate, saved_up=saved_up, w_down=w_down)


def slot_positions(block_routes):
    flat_routes = block_routes.reshape(-1).astype(jnp.int32)
    onehot = (flat_routes[:, None] == jnp.arange(EXPERTS, dtype=jnp.int32)[None, :]).astype(jnp.int32)
    before = jnp.cumsum(onehot, axis=0).astype(jnp.int32) - onehot
    slot = jnp.sum(before * onehot, axis=1).astype(jnp.int32)
    return (flat_routes * CAP + slot).astype(jnp.int32)


def build_block(position, rows, weights):
    repeated = jnp.repeat(rows, ROUTES, axis=0)
    sent_rows = jnp.zeros((EXPERTS * CAP, DW), rows.dtype).at[position].set(repeated)
    sent_weight = jnp.zeros((EXPERTS * CAP,), jnp.float32).at[position].set(weights.reshape(-1))
    return sent_rows.reshape(EXPERTS, CAP, DW), sent_weight.reshape(EXPERTS, CAP)


def owner_work(rows_in, weight_in, gate_in, up_in, matrix):
    rows = rows_in.reshape(-1, DW)
    weights = weight_in.reshape(-1)
    gate_pre = gate_in.reshape(-1, HID).astype(jnp.float32)
    up_pre = up_in.reshape(-1, HID).astype(jnp.float32)
    sigmoid_gate = jax.nn.sigmoid(gate_pre)
    hidden = (gate_pre * sigmoid_gate * up_pre).astype(jnp.bfloat16)
    weighted = (weights[:, None] * rows.astype(jnp.float32)).astype(jnp.bfloat16)
    partial_grad = jnp.dot(hidden.T, weighted, preferred_element_type=jnp.float32)
    back = jnp.dot(rows, matrix.T, preferred_element_type=jnp.float32)
    grad_hidden = weights[:, None] * back
    grad_gate = (grad_hidden * up_pre * sigmoid_gate * (1.0 + gate_pre * (1.0 - sigmoid_gate))).astype(jnp.bfloat16)
    grad_up = (grad_hidden * gate_pre * sigmoid_gate).astype(jnp.bfloat16)
    slot_grad = jnp.sum(hidden.astype(jnp.float32) * back, axis=1)
    return (partial_grad, grad_gate.reshape(EXPERTS, CAP, HID), grad_up.reshape(EXPERTS, CAP, HID),
            slot_grad.reshape(EXPERTS, CAP))


def reference(out_grad, combine_weight, routes, saved_gate, saved_up, w_down):
    blocks_rows = out_grad.reshape(EXPERTS * N_DP, TOK_DEV, DW)
    blocks_weight = combine_weight.reshape(EXPERTS * N_DP, TOK_DEV, ROUTES)
    blocks_routes = routes.reshape(EXPERTS * N_DP, TOK_DEV, ROUTES)

    def per_index(total, index):
        chosen = (jnp.arange(EXPERTS, dtype=jnp.int32) * N_DP + index).astype(jnp.int32)
        position = jax.vmap(slot_positions)(blocks_routes[chosen])
        sent_rows, sent_weight = jax.vmap(build_block)(position, blocks_rows[chosen], blocks_weight[chosen])
        sent_rows = jnp.swapaxes(sent_rows, 0, 1)
        sent_weight = jnp.swapaxes(sent_weight, 0, 1)
        partial_grad, grad_gate, grad_up, slot_grad = jax.vmap(owner_work)(
            sent_rows, sent_weight, saved_gate[:, index], saved_up[:, index], w_down)
        flat_grad = jnp.swapaxes(slot_grad, 0, 1).reshape(EXPERTS, EXPERTS * CAP)
        grad_combine = jnp.take_along_axis(flat_grad, position, axis=1).reshape(EXPERTS, TOK_DEV, ROUTES)
        return total + partial_grad, (grad_gate, grad_up, grad_combine)

    start = jnp.zeros((EXPERTS, HID, DW), jnp.float32)
    total, stacked = lax.scan(per_index, start, jnp.arange(N_DP, dtype=jnp.int32))
    grad_gate = jnp.transpose(stacked[0], (1, 0, 2, 3, 4))
    grad_up = jnp.transpose(stacked[1], (1, 0, 2, 3, 4))
    grad_combine = jnp.transpose(stacked[2], (1, 0, 2, 3)).reshape(TOKENS, ROUTES)
    return total, grad_gate, grad_up, grad_combine
```

```python
import jax
import jax.numpy as jnp
from jax import lax
from jax.sharding import PartitionSpec as P


def round_bf16(value):
    return lax.reduce_precision(value, exponent_bits=8, mantissa_bits=7)


def weight_pieces(weights):
    high = round_bf16(weights)
    rest = weights - high
    middle = round_bf16(rest)
    low = rest - middle
    return jnp.stack([high, middle, low], axis=-1).astype(jnp.bfloat16)


def local(out_grad, combine_weight, routes, saved_gate, saved_up, w_down):
    experts = lax.axis_size("expert")
    tok_rows, route_count = routes.shape
    capacity = saved_gate.shape[3]
    hidden_count = saved_gate.shape[4]
    feature_count = out_grad.shape[1]
    slots = experts * capacity
    lanes = 128

    flat_routes = routes.reshape(-1)
    route_total = flat_routes.shape[0]
    onehot = (flat_routes[:, None] == jnp.arange(experts, dtype=jnp.int32)[None, :]).astype(
        jnp.float32
    )
    order = jnp.arange(route_total, dtype=jnp.int32)
    earlier = (order[None, :] < order[:, None]).astype(jnp.bfloat16)
    before = jnp.dot(earlier, onehot.astype(jnp.bfloat16), preferred_element_type=jnp.float32)
    slot = jnp.sum(before * onehot, axis=1).astype(jnp.int32)
    position = flat_routes * capacity + slot

    slot_ids = jnp.arange(slots, dtype=jnp.int32)
    pick_route = position[None, :] == slot_ids[:, None]
    pick_token = pick_route.reshape(slots, tok_rows, route_count).any(axis=2)
    sent_rows = jnp.dot(
        pick_token.astype(out_grad.dtype), out_grad, preferred_element_type=jnp.float32
    ).astype(out_grad.dtype)
    pieces = weight_pieces(combine_weight.reshape(-1))
    pieces = jnp.pad(pieces, ((0, 0), (0, lanes - pieces.shape[1])))
    sent_pieces = jnp.dot(
        pick_route.astype(jnp.bfloat16), pieces, preferred_element_type=jnp.float32
    ).astype(jnp.bfloat16)
    packed = jnp.concatenate([sent_rows, sent_pieces], axis=1)
    arrived = lax.all_to_all(
        packed.reshape(experts, capacity, feature_count + lanes),
        "expert",
        split_axis=0,
        concat_axis=0,
        tiled=True,
    ).reshape(slots, feature_count + lanes)
    rows = arrived[:, :feature_count]
    got = arrived[:, feature_count:feature_count + 3].astype(jnp.float32)
    weights = (got[:, 0] + got[:, 1]) + got[:, 2]

    gate_pre = saved_gate.reshape(-1, hidden_count).astype(jnp.float32)
    up_pre = saved_up.reshape(-1, hidden_count).astype(jnp.float32)
    sigmoid_gate = jax.nn.sigmoid(gate_pre)
    hidden = (gate_pre * sigmoid_gate * up_pre).astype(jnp.bfloat16)
    weighted = (weights[:, None] * rows.astype(jnp.float32)).astype(jnp.bfloat16)
    partial_grad = lax.dot_general(
        hidden, weighted, (((0,), (0,)), ((), ())), preferred_element_type=jnp.float32
    )
    summed = lax.psum_scatter(
        partial_grad.astype(jnp.bfloat16), "dp", scatter_dimension=0, tiled=True
    )
    grad_weight = summed.astype(jnp.float32)

    matrix = w_down[0]
    back = lax.dot_general(
        rows, matrix, (((1,), (1,)), ((), ())), preferred_element_type=jnp.float32
    )
    grad_hidden = weights[:, None] * back
    grad_gate = (
        grad_hidden * up_pre * sigmoid_gate * (1.0 + gate_pre * (1.0 - sigmoid_gate))
    ).astype(jnp.bfloat16)
    grad_up = (grad_hidden * gate_pre * sigmoid_gate).astype(jnp.bfloat16)
    slot_grad = jnp.sum(hidden.astype(jnp.float32) * back, axis=1)
    returned = lax.all_to_all(
        slot_grad.reshape(experts, capacity), "expert", split_axis=0, concat_axis=0, tiled=True
    )
    grad_combine = returned.reshape(-1)[position].reshape(tok_rows, route_count)
    return (
        grad_weight[None],
        grad_gate.reshape(saved_gate.shape),
        grad_up.reshape(saved_up.shape),
        grad_combine,
    )


def solution(mesh):
    in_specs = (
        P(("expert", "dp"), None),
        P(("expert", "dp"), None),
        P(("expert", "dp"), None),
        P("expert", "dp", None, None, None),
        P("expert", "dp", None, None, None),
        P("expert", None, None),
    )
    out_specs = (
        P("expert", "dp", None),
        P("expert", "dp", None, None, None),
        P("expert", "dp", None, None, None),
        P(("expert", "dp"), None),
    )
    return jax.shard_map(local, mesh=mesh, in_specs=in_specs, out_specs=out_specs, check_vma=False)
```

```python
import jax
import jax.numpy as jnp
from jax import lax
from jax.sharding import PartitionSpec as P


CHUNKS = 4


def round_bf16(value):
    return lax.reduce_precision(value, exponent_bits=8, mantissa_bits=7)


def weight_pieces(weights):
    high = round_bf16(weights)
    rest = weights - high
    middle = round_bf16(rest)
    low = rest - middle
    return jnp.stack([high, middle, low], axis=-1).astype(jnp.bfloat16)


def local(out_grad, combine_weight, routes, saved_gate, saved_up, w_down):
    experts = lax.axis_size("expert")
    tok_rows, route_count = routes.shape
    capacity = saved_gate.shape[3]
    hidden_count = saved_gate.shape[4]
    feature_count = out_grad.shape[1]
    slots = experts * capacity
    lanes = 128

    flat_routes = routes.reshape(-1)
    route_total = flat_routes.shape[0]
    onehot = (flat_routes[:, None] == jnp.arange(experts, dtype=jnp.int32)[None, :]).astype(
        jnp.float32
    )
    order = jnp.arange(route_total, dtype=jnp.int32)
    earlier = (order[None, :] < order[:, None]).astype(jnp.bfloat16)
    before = jnp.dot(earlier, onehot.astype(jnp.bfloat16), preferred_element_type=jnp.float32)
    slot = jnp.sum(before * onehot, axis=1).astype(jnp.int32)
    position = flat_routes * capacity + slot

    slot_ids = jnp.arange(slots, dtype=jnp.int32)
    pick_route = position[None, :] == slot_ids[:, None]
    pick_token = pick_route.reshape(slots, tok_rows, route_count).any(axis=2)
    pieces = weight_pieces(combine_weight.reshape(-1))
    pieces = jnp.pad(pieces, ((0, 0), (0, lanes - pieces.shape[1])))
    sent_pieces = jnp.dot(
        pick_route.astype(jnp.bfloat16), pieces, preferred_element_type=jnp.float32
    ).astype(jnp.bfloat16)

    gate_pre = saved_gate.reshape(-1, hidden_count).astype(jnp.float32)
    up_pre = saved_up.reshape(-1, hidden_count).astype(jnp.float32)
    sigmoid_gate = jax.nn.sigmoid(gate_pre)
    hidden = (gate_pre * sigmoid_gate * up_pre).astype(jnp.bfloat16)

    def exchange(block):
        width = block.shape[1]
        return lax.all_to_all(
            block.reshape(experts, capacity, width), "expert",
            split_axis=0, concat_axis=0, tiled=True,
        ).reshape(slots, width)

    chunks = CHUNKS if feature_count % (CHUNKS * lanes) == 0 else 1
    width = feature_count // chunks
    row_parts, grad_parts = [], []
    weights = None
    pick_rows = pick_token.astype(out_grad.dtype)
    sends = [
        jnp.dot(
            pick_rows, out_grad[:, part * width:(part + 1) * width],
            preferred_element_type=jnp.float32,
        ).astype(out_grad.dtype)
        for part in range(chunks)
    ]
    sends[0] = jnp.concatenate([sends[0], sent_pieces], axis=1)
    for part in range(chunks):
        arrived = exchange(sends[part])
        if part == 0:
            rows_part = arrived[:, :width]
            got = arrived[:, width:width + 3].astype(jnp.float32)
            weights = (got[:, 0] + got[:, 1]) + got[:, 2]
        else:
            rows_part = arrived
        weighted = (weights[:, None] * rows_part.astype(jnp.float32)).astype(jnp.bfloat16)
        partial_grad = lax.dot_general(
            hidden, weighted, (((0,), (0,)), ((), ())), preferred_element_type=jnp.float32
        ).astype(jnp.bfloat16)
        if part + 1 < chunks:
            partial_grad, sends[part + 1] = lax.optimization_barrier(
                (partial_grad, sends[part + 1])
            )
        summed = lax.psum_scatter(partial_grad, "dp", scatter_dimension=0, tiled=True)
        row_parts.append(rows_part)
        grad_parts.append(summed.astype(jnp.float32))
    rows = jnp.concatenate(row_parts, axis=1) if chunks > 1 else row_parts[0]
    grad_weight = jnp.concatenate(grad_parts, axis=1) if chunks > 1 else grad_parts[0]

    matrix = w_down[0]
    back = lax.dot_general(
        rows, matrix, (((1,), (1,)), ((), ())), preferred_element_type=jnp.float32
    )
    grad_hidden = weights[:, None] * back
    grad_gate = (
        grad_hidden * up_pre * sigmoid_gate * (1.0 + gate_pre * (1.0 - sigmoid_gate))
    ).astype(jnp.bfloat16)
    grad_up = (grad_hidden * gate_pre * sigmoid_gate).astype(jnp.bfloat16)
    slot_grad = jnp.sum(hidden.astype(jnp.float32) * back, axis=1)
    returned = lax.all_to_all(
        slot_grad.reshape(experts, capacity), "expert", split_axis=0, concat_axis=0, tiled=True
    )
    grad_combine = returned.reshape(-1)[position].reshape(tok_rows, route_count)
    return (
        grad_weight[None],
        grad_gate.reshape(saved_gate.shape),
        grad_up.reshape(saved_up.shape),
        grad_combine,
    )


def solution(mesh):
    in_specs = (
        P(("expert", "dp"), None),
        P(("expert", "dp"), None),
        P(("expert", "dp"), None),
        P("expert", "dp", None, None, None),
        P("expert", "dp", None, None, None),
        P("expert", None, None),
    )
    out_specs = (
        P("expert", "dp", None),
        P("expert", "dp", None, None, None),
        P("expert", "dp", None, None, None),
        P(("expert", "dp"), None),
    )
    return jax.shard_map(local, mesh=mesh, in_specs=in_specs, out_specs=out_specs, check_vma=False)
```

```python
import jax
import jax.numpy as jnp
from jax import lax
from jax.sharding import PartitionSpec as P


def round_bf16(value):
    return lax.reduce_precision(value, exponent_bits=8, mantissa_bits=7)


def weight_pieces(weights):
    high = round_bf16(weights)
    rest = weights - high
    middle = round_bf16(rest)
    low = rest - middle
    return jnp.stack([high, middle, low], axis=-1).astype(jnp.bfloat16)


def local(out_grad, combine_weight, routes, saved_gate, saved_up, w_down):
    experts = lax.axis_size("expert")
    tok_rows, route_count = routes.shape
    capacity = saved_gate.shape[3]
    hidden_count = saved_gate.shape[4]
    feature_count = out_grad.shape[1]
    slots = experts * capacity
    lanes = 128

    flat_routes = routes.reshape(-1)
    route_total = flat_routes.shape[0]
    onehot = (flat_routes[:, None] == jnp.arange(experts, dtype=jnp.int32)[None, :]).astype(
        jnp.float32
    )
    order = jnp.arange(route_total, dtype=jnp.int32)
    earlier = (order[None, :] < order[:, None]).astype(jnp.bfloat16)
    before = jnp.dot(earlier, onehot.astype(jnp.bfloat16), preferred_element_type=jnp.float32)
    slot = jnp.sum(before * onehot, axis=1).astype(jnp.int32)
    position = flat_routes * capacity + slot

    slot_ids = jnp.arange(slots, dtype=jnp.int32)
    pick_route = position[None, :] == slot_ids[:, None]
    pick_token = pick_route.reshape(slots, tok_rows, route_count).any(axis=2)
    sent_rows = jnp.dot(
        pick_token.astype(out_grad.dtype), out_grad, preferred_element_type=jnp.float32
    ).astype(out_grad.dtype)
    pieces = weight_pieces(combine_weight.reshape(-1))
    pieces = jnp.pad(pieces, ((0, 0), (0, lanes - pieces.shape[1])))
    sent_pieces = jnp.dot(
        pick_route.astype(jnp.bfloat16), pieces, preferred_element_type=jnp.float32
    ).astype(jnp.bfloat16)
    packed = jnp.concatenate([sent_rows, sent_pieces], axis=1)
    arrived = lax.all_to_all(
        packed.reshape(experts, capacity, feature_count + lanes),
        "expert",
        split_axis=0,
        concat_axis=0,
        tiled=True,
    ).reshape(slots, feature_count + lanes)
    rows = arrived[:, :feature_count]
    got = arrived[:, feature_count:feature_count + 3].astype(jnp.float32)
    weights = (got[:, 0] + got[:, 1]) + got[:, 2]

    gate_pre = saved_gate.reshape(-1, hidden_count).astype(jnp.float32)
    up_pre = saved_up.reshape(-1, hidden_count).astype(jnp.float32)
    sigmoid_gate = jax.nn.sigmoid(gate_pre)
    hidden = (gate_pre * sigmoid_gate * up_pre).astype(jnp.bfloat16)
    weighted = (weights[:, None] * rows.astype(jnp.float32)).astype(jnp.bfloat16)
    chips = lax.axis_size("z")
    cores = lax.axis_size("core")
    share = hidden_count // (chips * cores)
    hidden_order = (
        hidden.reshape(-1, chips, cores, share).transpose(0, 2, 1, 3).reshape(-1, hidden_count)
    )
    partial_grad = lax.dot_general(
        hidden_order, weighted, (((0,), (0,)), ((), ())), preferred_element_type=jnp.float32
    )
    on_chip = lax.psum_scatter(
        partial_grad.astype(jnp.bfloat16), "core", scatter_dimension=0, tiled=True
    )
    summed = lax.psum_scatter(on_chip, "z", scatter_dimension=0, tiled=True)
    grad_weight = summed.astype(jnp.float32)

    matrix = w_down[0]
    back = lax.dot_general(
        rows, matrix, (((1,), (1,)), ((), ())), preferred_element_type=jnp.float32
    )
    grad_hidden = weights[:, None] * back
    grad_gate = (
        grad_hidden * up_pre * sigmoid_gate * (1.0 + gate_pre * (1.0 - sigmoid_gate))
    ).astype(jnp.bfloat16)
    grad_up = (grad_hidden * gate_pre * sigmoid_gate).astype(jnp.bfloat16)
    slot_grad = jnp.sum(hidden.astype(jnp.float32) * back, axis=1)
    returned = lax.all_to_all(
        slot_grad.reshape(experts, capacity), "expert", split_axis=0, concat_axis=0, tiled=True
    )
    grad_combine = returned.reshape(-1)[position].reshape(tok_rows, route_count)
    return (
        grad_weight[None],
        grad_gate.reshape(saved_gate.shape),
        grad_up.reshape(saved_up.shape),
        grad_combine,
    )


def solution(mesh):
    experts, data = mesh.devices.shape
    cores = 2
    mesh = jax.sharding.Mesh(
        mesh.devices.reshape(experts, data // cores, cores), ("expert", "z", "core")
    )
    in_specs = (
        P(("expert", "z", "core"), None),
        P(("expert", "z", "core"), None),
        P(("expert", "z", "core"), None),
        P("expert", ("z", "core"), None, None, None),
        P("expert", ("z", "core"), None, None, None),
        P("expert", None, None),
    )
    out_specs = (
        P("expert", ("z", "core"), None),
        P("expert", ("z", "core"), None, None, None),
        P("expert", ("z", "core"), None, None, None),
        P(("expert", "z", "core"), None),
    )
    return jax.shard_map(local, mesh=mesh, in_specs=in_specs, out_specs=out_specs, check_vma=False)
```

```python
import jax
import jax.numpy as jnp
from jax import lax
from jax.sharding import PartitionSpec as P


def round_bf16(value):
    return lax.reduce_precision(value, exponent_bits=8, mantissa_bits=7)


def weight_pieces(weights):
    high = round_bf16(weights)
    rest = weights - high
    middle = round_bf16(rest)
    low = rest - middle
    return jnp.stack([high, middle, low], axis=-1).astype(jnp.bfloat16)


def pick(blocks, index):
    return lax.dynamic_index_in_dim(blocks, index, axis=0, keepdims=False)


def line_scatter(partial):
    chips = lax.axis_size("z")
    cores = lax.axis_size("core")
    features = partial.shape[1]
    share = partial.shape[0] // (chips * cores)
    if chips > 4 or cores != 2:
        summed = lax.psum_scatter(
            partial.astype(jnp.bfloat16), ("z", "core"), scatter_dimension=0, tiled=True
        )
        return summed.astype(jnp.float32)
    blocks = jnp.swapaxes(partial.reshape(chips, cores, share, features), 0, 1)
    core = lax.axis_index("core")
    outgoing = pick(blocks, 1 - core).astype(jnp.bfloat16)
    incoming = lax.ppermute(outgoing, "core", perm=[(0, 1), (1, 0)])
    mine = pick(blocks, core) + incoming.astype(jnp.float32)
    chip = lax.axis_index("z")
    right = jnp.zeros((share, features), jnp.bfloat16)
    left = jnp.zeros((share, features), jnp.bfloat16)
    for step in range(1, chips):
        send_right = pick(mine, chip + chips - step) + right.astype(jnp.float32)
        send_left = pick(mine, chip - chips + step) + left.astype(jnp.float32)
        right = lax.ppermute(
            send_right.astype(jnp.bfloat16), "z",
            perm=[(k, k + 1) for k in range(step) if k + 1 < chips],
        )
        left = lax.ppermute(
            send_left.astype(jnp.bfloat16), "z",
            perm=[(chips - 1 - k, chips - 2 - k) for k in range(step) if chips - 2 - k >= 0],
        )
    return pick(mine, chip) + right.astype(jnp.float32) + left.astype(jnp.float32)


def local(out_grad, combine_weight, routes, saved_gate, saved_up, w_down):
    experts = lax.axis_size("expert")
    tok_rows, route_count = routes.shape
    capacity = saved_gate.shape[3]
    hidden_count = saved_gate.shape[4]
    feature_count = out_grad.shape[1]
    slots = experts * capacity
    lanes = 128

    flat_routes = routes.reshape(-1)
    route_total = flat_routes.shape[0]
    onehot = (flat_routes[:, None] == jnp.arange(experts, dtype=jnp.int32)[None, :]).astype(
        jnp.float32
    )
    order = jnp.arange(route_total, dtype=jnp.int32)
    earlier = (order[None, :] < order[:, None]).astype(jnp.bfloat16)
    before = jnp.dot(earlier, onehot.astype(jnp.bfloat16), preferred_element_type=jnp.float32)
    slot = jnp.sum(before * onehot, axis=1).astype(jnp.int32)
    position = flat_routes * capacity + slot

    slot_ids = jnp.arange(slots, dtype=jnp.int32)
    pick_route = position[None, :] == slot_ids[:, None]
    pick_token = pick_route.reshape(slots, tok_rows, route_count).any(axis=2)
    sent_rows = jnp.dot(
        pick_token.astype(out_grad.dtype), out_grad, preferred_element_type=jnp.float32
    ).astype(out_grad.dtype)
    pieces = weight_pieces(combine_weight.reshape(-1))
    pieces = jnp.pad(pieces, ((0, 0), (0, lanes - pieces.shape[1])))
    sent_pieces = jnp.dot(
        pick_route.astype(jnp.bfloat16), pieces, preferred_element_type=jnp.float32
    ).astype(jnp.bfloat16)
    packed = jnp.concatenate([sent_rows, sent_pieces], axis=1)
    arrived = lax.all_to_all(
        packed.reshape(experts, capacity, feature_count + lanes),
        "expert",
        split_axis=0,
        concat_axis=0,
        tiled=True,
    ).reshape(slots, feature_count + lanes)
    rows = arrived[:, :feature_count]
    got = arrived[:, feature_count:feature_count + 3].astype(jnp.float32)
    weights = (got[:, 0] + got[:, 1]) + got[:, 2]

    gate_pre = saved_gate.reshape(-1, hidden_count).astype(jnp.float32)
    up_pre = saved_up.reshape(-1, hidden_count).astype(jnp.float32)
    sigmoid_gate = jax.nn.sigmoid(gate_pre)
    hidden = (gate_pre * sigmoid_gate * up_pre).astype(jnp.bfloat16)
    weighted = (weights[:, None] * rows.astype(jnp.float32)).astype(jnp.bfloat16)
    partial_grad = lax.dot_general(
        hidden, weighted, (((0,), (0,)), ((), ())), preferred_element_type=jnp.float32
    )
    grad_weight = line_scatter(partial_grad)

    matrix = w_down[0]
    back = lax.dot_general(
        rows, matrix, (((1,), (1,)), ((), ())), preferred_element_type=jnp.float32
    )
    grad_hidden = weights[:, None] * back
    grad_gate = (
        grad_hidden * up_pre * sigmoid_gate * (1.0 + gate_pre * (1.0 - sigmoid_gate))
    ).astype(jnp.bfloat16)
    grad_up = (grad_hidden * gate_pre * sigmoid_gate).astype(jnp.bfloat16)
    slot_grad = jnp.sum(hidden.astype(jnp.float32) * back, axis=1)
    returned = lax.all_to_all(
        slot_grad.reshape(experts, capacity), "expert", split_axis=0, concat_axis=0, tiled=True
    )
    grad_combine = returned.reshape(-1)[position].reshape(tok_rows, route_count)
    return (
        grad_weight[None],
        grad_gate.reshape(saved_gate.shape),
        grad_up.reshape(saved_up.shape),
        grad_combine,
    )


def solution(mesh):
    experts, data = mesh.devices.shape
    cores = 2
    mesh = jax.sharding.Mesh(
        mesh.devices.reshape(experts, data // cores, cores), ("expert", "z", "core")
    )
    in_specs = (
        P(("expert", "z", "core"), None),
        P(("expert", "z", "core"), None),
        P(("expert", "z", "core"), None),
        P("expert", ("z", "core"), None, None, None),
        P("expert", ("z", "core"), None, None, None),
        P("expert", None, None),
    )
    out_specs = (
        P("expert", ("z", "core"), None),
        P("expert", ("z", "core"), None, None, None),
        P("expert", ("z", "core"), None, None, None),
        P(("expert", "z", "core"), None),
    )
    return jax.shard_map(local, mesh=mesh, in_specs=in_specs, out_specs=out_specs, check_vma=False)
```

```python
import jax
import jax.numpy as jnp
from jax import lax
from jax.sharding import PartitionSpec as P


def round_bf16(value):
    return lax.reduce_precision(value, exponent_bits=8, mantissa_bits=7)


def weight_pieces(weights):
    high = round_bf16(weights)
    rest = weights - high
    middle = round_bf16(rest)
    low = rest - middle
    return jnp.stack([high, middle, low], axis=-1).astype(jnp.bfloat16)


def local(out_grad, combine_weight, routes, saved_gate, saved_up, w_down):
    experts = lax.axis_size("expert")
    tok_rows, route_count = routes.shape
    capacity = saved_gate.shape[3]
    hidden_count = saved_gate.shape[4]
    feature_count = out_grad.shape[1]
    slots = experts * capacity
    lanes = 128

    flat_routes = routes.reshape(-1)
    route_total = flat_routes.shape[0]
    onehot = (flat_routes[:, None] == jnp.arange(experts, dtype=jnp.int32)[None, :]).astype(
        jnp.float32
    )
    order = jnp.arange(route_total, dtype=jnp.int32)
    earlier = (order[None, :] < order[:, None]).astype(jnp.bfloat16)
    before = jnp.dot(earlier, onehot.astype(jnp.bfloat16), preferred_element_type=jnp.float32)
    slot = jnp.sum(before * onehot, axis=1).astype(jnp.int32)
    position = flat_routes * capacity + slot

    slot_ids = jnp.arange(slots, dtype=jnp.int32)
    pick_route = position[None, :] == slot_ids[:, None]
    pick_token = pick_route.reshape(slots, tok_rows, route_count).any(axis=2)
    sent_rows = jnp.dot(
        pick_token.astype(out_grad.dtype), out_grad, preferred_element_type=jnp.float32
    ).astype(out_grad.dtype)
    pieces = weight_pieces(combine_weight.reshape(-1))
    pieces = jnp.pad(pieces, ((0, 0), (0, lanes - pieces.shape[1])))
    sent_pieces = jnp.dot(
        pick_route.astype(jnp.bfloat16), pieces, preferred_element_type=jnp.float32
    ).astype(jnp.bfloat16)
    packed = jnp.concatenate([sent_rows, sent_pieces], axis=1)
    arrived = lax.all_to_all(
        packed.reshape(experts, capacity, feature_count + lanes),
        "expert",
        split_axis=0,
        concat_axis=0,
        tiled=True,
    ).reshape(slots, feature_count + lanes)
    rows = arrived[:, :feature_count]
    got = arrived[:, feature_count:feature_count + 3].astype(jnp.float32)
    weights = (got[:, 0] + got[:, 1]) + got[:, 2]

    gate_pre = saved_gate.reshape(-1, hidden_count).astype(jnp.float32)
    up_pre = saved_up.reshape(-1, hidden_count).astype(jnp.float32)
    sigmoid_gate = jax.nn.sigmoid(gate_pre)
    hidden = (gate_pre * sigmoid_gate * up_pre).astype(jnp.bfloat16)
    weighted = (weights[:, None] * rows.astype(jnp.float32)).astype(jnp.bfloat16)
    partial_grad = lax.dot_general(
        hidden, weighted, (((0,), (0,)), ((), ())), preferred_element_type=jnp.float32
    )
    partial_grad, rows = lax.optimization_barrier((partial_grad.astype(jnp.bfloat16), rows))
    summed = lax.psum_scatter(partial_grad, "dp", scatter_dimension=0, tiled=True)
    grad_weight = summed.astype(jnp.float32)

    matrix = w_down[0]
    back = lax.dot_general(
        rows, matrix, (((1,), (1,)), ((), ())), preferred_element_type=jnp.float32
    )
    grad_hidden = weights[:, None] * back
    grad_gate = (
        grad_hidden * up_pre * sigmoid_gate * (1.0 + gate_pre * (1.0 - sigmoid_gate))
    ).astype(jnp.bfloat16)
    grad_up = (grad_hidden * gate_pre * sigmoid_gate).astype(jnp.bfloat16)
    slot_grad = jnp.sum(hidden.astype(jnp.float32) * back, axis=1)
    returned = lax.all_to_all(
        slot_grad.reshape(experts, capacity), "expert", split_axis=0, concat_axis=0, tiled=True
    )
    grad_combine = returned.reshape(-1)[position].reshape(tok_rows, route_count)
    return (
        grad_weight[None],
        grad_gate.reshape(saved_gate.shape),
        grad_up.reshape(saved_up.shape),
        grad_combine,
    )


def solution(mesh):
    in_specs = (
        P(("expert", "dp"), None),
        P(("expert", "dp"), None),
        P(("expert", "dp"), None),
        P("expert", "dp", None, None, None),
        P("expert", "dp", None, None, None),
        P("expert", None, None),
    )
    out_specs = (
        P("expert", "dp", None),
        P("expert", "dp", None, None, None),
        P("expert", "dp", None, None, None),
        P(("expert", "dp"), None),
    )
    return jax.shard_map(local, mesh=mesh, in_specs=in_specs, out_specs=out_specs, check_vma=False)
```

```python
import jax
import jax.numpy as jnp
from jax import lax
from jax.sharding import PartitionSpec as P


def round_bf16(value):
    return lax.reduce_precision(value, exponent_bits=8, mantissa_bits=7)


def weight_pieces(weights):
    high = round_bf16(weights)
    rest = weights - high
    middle = round_bf16(rest)
    low = rest - middle
    return jnp.stack([high, middle, low], axis=-1).astype(jnp.bfloat16)


def local(out_grad, combine_weight, routes, saved_gate, saved_up, w_down):
    experts = lax.axis_size("expert")
    tok_rows, route_count = routes.shape
    capacity = saved_gate.shape[3]
    hidden_count = saved_gate.shape[4]
    feature_count = out_grad.shape[1]
    slots = experts * capacity
    lanes = 128

    flat_routes = routes.reshape(-1)
    route_total = flat_routes.shape[0]
    onehot = (flat_routes[:, None] == jnp.arange(experts, dtype=jnp.int32)[None, :]).astype(
        jnp.float32
    )
    order = jnp.arange(route_total, dtype=jnp.int32)
    earlier = (order[None, :] < order[:, None]).astype(jnp.bfloat16)
    before = jnp.dot(earlier, onehot.astype(jnp.bfloat16), preferred_element_type=jnp.float32)
    slot = jnp.sum(before * onehot, axis=1).astype(jnp.int32)
    position = flat_routes * capacity + slot

    slot_ids = jnp.arange(slots, dtype=jnp.int32)
    pick_route = position[None, :] == slot_ids[:, None]
    pick_token = pick_route.reshape(slots, tok_rows, route_count).any(axis=2)
    sent_rows = jnp.dot(
        pick_token.astype(out_grad.dtype), out_grad, preferred_element_type=jnp.float32
    ).astype(out_grad.dtype)
    pieces = weight_pieces(combine_weight.reshape(-1))
    pieces = jnp.pad(pieces, ((0, 0), (0, lanes - pieces.shape[1])))
    sent_pieces = jnp.dot(
        pick_route.astype(jnp.bfloat16), pieces, preferred_element_type=jnp.float32
    ).astype(jnp.bfloat16)
    packed = jnp.concatenate([sent_rows, sent_pieces], axis=1)
    arrived = lax.all_to_all(
        packed.reshape(experts, capacity, feature_count + lanes),
        "expert",
        split_axis=0,
        concat_axis=0,
        tiled=True,
    ).reshape(slots, feature_count + lanes)
    rows = arrived[:, :feature_count]
    got = arrived[:, feature_count:feature_count + 3].astype(jnp.float32)
    weights = (got[:, 0] + got[:, 1]) + got[:, 2]

    gate_pre = saved_gate.reshape(-1, hidden_count).astype(jnp.float32)
    up_pre = saved_up.reshape(-1, hidden_count).astype(jnp.float32)
    sigmoid_gate = jax.nn.sigmoid(gate_pre)
    hidden = (gate_pre * sigmoid_gate * up_pre).astype(jnp.bfloat16)
    weighted = (weights[:, None] * rows.astype(jnp.float32)).astype(jnp.bfloat16)
    partial_grad = lax.dot_general(
        hidden, weighted, (((0,), (0,)), ((), ())), preferred_element_type=jnp.float32
    )
    partial_grad, arrived = lax.optimization_barrier(
        (partial_grad.astype(jnp.bfloat16), arrived)
    )
    rows = arrived[:, :feature_count]
    summed = lax.psum_scatter(partial_grad, "dp", scatter_dimension=0, tiled=True)
    grad_weight = summed.astype(jnp.float32)

    matrix = w_down[0]
    back = lax.dot_general(
        rows, matrix, (((1,), (1,)), ((), ())), preferred_element_type=jnp.float32
    )
    grad_hidden = weights[:, None] * back
    grad_gate = (
        grad_hidden * up_pre * sigmoid_gate * (1.0 + gate_pre * (1.0 - sigmoid_gate))
    ).astype(jnp.bfloat16)
    grad_up = (grad_hidden * gate_pre * sigmoid_gate).astype(jnp.bfloat16)
    slot_grad = jnp.sum(hidden.astype(jnp.float32) * back, axis=1)
    returned = lax.all_to_all(
        slot_grad.reshape(experts, capacity), "expert", split_axis=0, concat_axis=0, tiled=True
    )
    grad_combine = returned.reshape(-1)[position].reshape(tok_rows, route_count)
    return (
        grad_weight[None],
        grad_gate.reshape(saved_gate.shape),
        grad_up.reshape(saved_up.shape),
        grad_combine,
    )


def solution(mesh):
    in_specs = (
        P(("expert", "dp"), None),
        P(("expert", "dp"), None),
        P(("expert", "dp"), None),
        P("expert", "dp", None, None, None),
        P("expert", "dp", None, None, None),
        P("expert", None, None),
    )
    out_specs = (
        P("expert", "dp", None),
        P("expert", "dp", None, None, None),
        P("expert", "dp", None, None, None),
        P(("expert", "dp"), None),
    )
    return jax.shard_map(local, mesh=mesh, in_specs=in_specs, out_specs=out_specs, check_vma=False)
```

```python
import jax
import jax.numpy as jnp
from jax import lax
from jax.sharding import PartitionSpec as P
from jax.experimental import pallas as pl
from jax.experimental.pallas import tpu as pltpu


def round_bf16(value):
    return lax.reduce_precision(value, exponent_bits=8, mantissa_bits=7)


def weight_pieces(weights):
    high = round_bf16(weights)
    rest = weights - high
    middle = round_bf16(rest)
    low = rest - middle
    return jnp.stack([high, middle, low], axis=-1).astype(jnp.bfloat16)


def partial_kernel(arrived_ref, gate_ref, up_ref, partial_ref, hidden_ref):
    features = partial_ref.shape[1]
    gate = gate_ref[...].astype(jnp.float32)
    sigmoid_gate = 1.0 / (1.0 + jnp.exp(-gate))
    hidden = (gate * sigmoid_gate * up_ref[...].astype(jnp.float32)).astype(jnp.bfloat16)
    hidden_ref[...] = hidden
    hidden_t = jnp.transpose(hidden.astype(jnp.float32)).astype(jnp.bfloat16)
    got = arrived_ref[:, features:features + 128].astype(jnp.float32)
    weights = (got[:, 0:1] + got[:, 1:2]) + got[:, 2:3]
    tile = 512 if features % 512 == 0 else features
    for start in range(0, features, tile):
        rows = arrived_ref[:, start:start + tile].astype(jnp.float32)
        weighted = (weights * rows).astype(jnp.bfloat16)
        partial_ref[:, start:start + tile] = jnp.dot(
            hidden_t, weighted, preferred_element_type=jnp.float32
        ).astype(jnp.bfloat16)


def weighted_partial(arrived, gate, up, features):
    slots, hidden_count = gate.shape
    vmem = pl.BlockSpec(memory_space=pltpu.VMEM)
    flops = 2 * slots * hidden_count * features
    moved = 2 * (arrived.size + 2 * gate.size + hidden_count * features + gate.size)
    return pl.pallas_call(
        partial_kernel,
        out_shape=(
            jax.ShapeDtypeStruct((hidden_count, features), jnp.bfloat16),
            jax.ShapeDtypeStruct((slots, hidden_count), jnp.bfloat16),
        ),
        in_specs=[vmem, vmem, vmem],
        out_specs=(vmem, vmem),
        cost_estimate=pl.CostEstimate(
            flops=flops, bytes_accessed=moved, transcendentals=gate.size
        ),
    )(arrived, gate, up)


def local(out_grad, combine_weight, routes, saved_gate, saved_up, w_down):
    experts = lax.axis_size("expert")
    tok_rows, route_count = routes.shape
    capacity = saved_gate.shape[3]
    hidden_count = saved_gate.shape[4]
    feature_count = out_grad.shape[1]
    slots = experts * capacity
    lanes = 128

    flat_routes = routes.reshape(-1)
    route_total = flat_routes.shape[0]
    onehot = (flat_routes[:, None] == jnp.arange(experts, dtype=jnp.int32)[None, :]).astype(
        jnp.float32
    )
    order = jnp.arange(route_total, dtype=jnp.int32)
    earlier = (order[None, :] < order[:, None]).astype(jnp.bfloat16)
    before = jnp.dot(earlier, onehot.astype(jnp.bfloat16), preferred_element_type=jnp.float32)
    slot = jnp.sum(before * onehot, axis=1).astype(jnp.int32)
    position = flat_routes * capacity + slot

    slot_ids = jnp.arange(slots, dtype=jnp.int32)
    pick_route = position[None, :] == slot_ids[:, None]
    pick_token = pick_route.reshape(slots, tok_rows, route_count).any(axis=2)
    sent_rows = jnp.dot(
        pick_token.astype(out_grad.dtype), out_grad, preferred_element_type=jnp.float32
    ).astype(out_grad.dtype)
    pieces = weight_pieces(combine_weight.reshape(-1))
    pieces = jnp.pad(pieces, ((0, 0), (0, lanes - pieces.shape[1])))
    sent_pieces = jnp.dot(
        pick_route.astype(jnp.bfloat16), pieces, preferred_element_type=jnp.float32
    ).astype(jnp.bfloat16)
    packed = jnp.concatenate([sent_rows, sent_pieces], axis=1)
    arrived = lax.all_to_all(
        packed.reshape(experts, capacity, feature_count + lanes),
        "expert",
        split_axis=0,
        concat_axis=0,
        tiled=True,
    ).reshape(slots, feature_count + lanes)
    rows = arrived[:, :feature_count]
    got = arrived[:, feature_count:feature_count + 3].astype(jnp.float32)
    weights = (got[:, 0] + got[:, 1]) + got[:, 2]

    gate_bf = saved_gate.reshape(-1, hidden_count)
    up_bf = saved_up.reshape(-1, hidden_count)
    partial_grad, hidden = weighted_partial(arrived, gate_bf, up_bf, feature_count)
    summed = lax.psum_scatter(partial_grad, "dp", scatter_dimension=0, tiled=True)
    gate_pre = gate_bf.astype(jnp.float32)
    up_pre = up_bf.astype(jnp.float32)
    sigmoid_gate = jax.nn.sigmoid(gate_pre)
    grad_weight = summed.astype(jnp.float32)

    matrix = w_down[0]
    back = lax.dot_general(
        rows, matrix, (((1,), (1,)), ((), ())), preferred_element_type=jnp.float32
    )
    grad_hidden = weights[:, None] * back
    grad_gate = (
        grad_hidden * up_pre * sigmoid_gate * (1.0 + gate_pre * (1.0 - sigmoid_gate))
    ).astype(jnp.bfloat16)
    grad_up = (grad_hidden * gate_pre * sigmoid_gate).astype(jnp.bfloat16)
    slot_grad = jnp.sum(hidden.astype(jnp.float32) * back, axis=1)
    returned = lax.all_to_all(
        slot_grad.reshape(experts, capacity), "expert", split_axis=0, concat_axis=0, tiled=True
    )
    grad_combine = returned.reshape(-1)[position].reshape(tok_rows, route_count)
    return (
        grad_weight[None],
        grad_gate.reshape(saved_gate.shape),
        grad_up.reshape(saved_up.shape),
        grad_combine,
    )


def solution(mesh):
    in_specs = (
        P(("expert", "dp"), None),
        P(("expert", "dp"), None),
        P(("expert", "dp"), None),
        P("expert", "dp", None, None, None),
        P("expert", "dp", None, None, None),
        P("expert", None, None),
    )
    out_specs = (
        P("expert", "dp", None),
        P("expert", "dp", None, None, None),
        P("expert", "dp", None, None, None),
        P(("expert", "dp"), None),
    )
    return jax.shard_map(local, mesh=mesh, in_specs=in_specs, out_specs=out_specs, check_vma=False)
```

```python
import jax
import jax.numpy as jnp
from jax import lax
from jax.sharding import PartitionSpec as P
from jax.experimental import pallas as pl
from jax.experimental.pallas import tpu as pltpu


def round_bf16(value):
    return lax.reduce_precision(value, exponent_bits=8, mantissa_bits=7)


def weight_pieces(weights):
    high = round_bf16(weights)
    rest = weights - high
    middle = round_bf16(rest)
    low = rest - middle
    return jnp.stack([high, middle, low], axis=-1).astype(jnp.bfloat16)


def partial_kernel(rows_ref, pieces_ref, gate_ref, up_ref, partial_ref, hidden_ref, hidden_t_ref):
    @pl.when(pl.program_id(0) == 0)
    def _():
        gate = gate_ref[...].astype(jnp.float32)
        sigmoid_gate = 1.0 / (1.0 + jnp.exp(-gate))
        hidden = (gate * sigmoid_gate * up_ref[...].astype(jnp.float32)).astype(jnp.bfloat16)
        hidden_ref[...] = hidden
        hidden_t_ref[...] = jnp.transpose(hidden.astype(jnp.float32)).astype(jnp.bfloat16)

    got = pieces_ref[...].astype(jnp.float32)
    weights = (got[:, 0:1] + got[:, 1:2]) + got[:, 2:3]
    weighted = (weights * rows_ref[...].astype(jnp.float32)).astype(jnp.bfloat16)
    partial_ref[...] = jnp.dot(
        hidden_t_ref[...], weighted, preferred_element_type=jnp.float32
    ).astype(jnp.bfloat16)


def weighted_partial(arrived, gate, up, features):
    slots, hidden_count = gate.shape
    lanes = arrived.shape[1] - features
    tile = 512 if features % 512 == 0 else features
    flops = 2 * slots * hidden_count * features
    moved = 2 * (arrived.size + 2 * gate.size + hidden_count * features + gate.size)
    return pl.pallas_call(
        partial_kernel,
        grid=(features // tile,),
        out_shape=(
            jax.ShapeDtypeStruct((hidden_count, features), jnp.bfloat16),
            jax.ShapeDtypeStruct((slots, hidden_count), jnp.bfloat16),
        ),
        in_specs=[
            pl.BlockSpec((slots, tile), lambda j: (0, j)),
            pl.BlockSpec((slots, lanes), lambda j: (0, features // lanes)),
            pl.BlockSpec((slots, hidden_count), lambda j: (0, 0)),
            pl.BlockSpec((slots, hidden_count), lambda j: (0, 0)),
        ],
        out_specs=(
            pl.BlockSpec((hidden_count, tile), lambda j: (0, j)),
            pl.BlockSpec((slots, hidden_count), lambda j: (0, 0)),
        ),
        scratch_shapes=[pltpu.VMEM((hidden_count, slots), jnp.bfloat16)],
        compiler_params=pltpu.CompilerParams(dimension_semantics=("arbitrary",)),
        cost_estimate=pl.CostEstimate(
            flops=flops, bytes_accessed=moved, transcendentals=gate.size
        ),
    )(arrived, arrived, gate, up)


def local(out_grad, combine_weight, routes, saved_gate, saved_up, w_down):
    experts = lax.axis_size("expert")
    tok_rows, route_count = routes.shape
    capacity = saved_gate.shape[3]
    hidden_count = saved_gate.shape[4]
    feature_count = out_grad.shape[1]
    slots = experts * capacity
    lanes = 128

    flat_routes = routes.reshape(-1)
    route_total = flat_routes.shape[0]
    onehot = (flat_routes[:, None] == jnp.arange(experts, dtype=jnp.int32)[None, :]).astype(
        jnp.float32
    )
    order = jnp.arange(route_total, dtype=jnp.int32)
    earlier = (order[None, :] < order[:, None]).astype(jnp.bfloat16)
    before = jnp.dot(earlier, onehot.astype(jnp.bfloat16), preferred_element_type=jnp.float32)
    slot = jnp.sum(before * onehot, axis=1).astype(jnp.int32)
    position = flat_routes * capacity + slot

    slot_ids = jnp.arange(slots, dtype=jnp.int32)
    pick_route = position[None, :] == slot_ids[:, None]
    pick_token = pick_route.reshape(slots, tok_rows, route_count).any(axis=2)
    sent_rows = jnp.dot(
        pick_token.astype(out_grad.dtype), out_grad, preferred_element_type=jnp.float32
    ).astype(out_grad.dtype)
    pieces = weight_pieces(combine_weight.reshape(-1))
    pieces = jnp.pad(pieces, ((0, 0), (0, lanes - pieces.shape[1])))
    sent_pieces = jnp.dot(
        pick_route.astype(jnp.bfloat16), pieces, preferred_element_type=jnp.float32
    ).astype(jnp.bfloat16)
    packed = jnp.concatenate([sent_rows, sent_pieces], axis=1)
    arrived = lax.all_to_all(
        packed.reshape(experts, capacity, feature_count + lanes),
        "expert",
        split_axis=0,
        concat_axis=0,
        tiled=True,
    ).reshape(slots, feature_count + lanes)
    rows = arrived[:, :feature_count]
    got = arrived[:, feature_count:feature_count + 3].astype(jnp.float32)
    weights = (got[:, 0] + got[:, 1]) + got[:, 2]

    gate_bf = saved_gate.reshape(-1, hidden_count)
    up_bf = saved_up.reshape(-1, hidden_count)
    partial_grad, hidden = weighted_partial(arrived, gate_bf, up_bf, feature_count)
    summed = lax.psum_scatter(partial_grad, "dp", scatter_dimension=0, tiled=True)
    gate_pre = gate_bf.astype(jnp.float32)
    up_pre = up_bf.astype(jnp.float32)
    sigmoid_gate = jax.nn.sigmoid(gate_pre)
    grad_weight = summed.astype(jnp.float32)

    matrix = w_down[0]
    back = lax.dot_general(
        rows, matrix, (((1,), (1,)), ((), ())), preferred_element_type=jnp.float32
    )
    grad_hidden = weights[:, None] * back
    grad_gate = (
        grad_hidden * up_pre * sigmoid_gate * (1.0 + gate_pre * (1.0 - sigmoid_gate))
    ).astype(jnp.bfloat16)
    grad_up = (grad_hidden * gate_pre * sigmoid_gate).astype(jnp.bfloat16)
    slot_grad = jnp.sum(hidden.astype(jnp.float32) * back, axis=1)
    returned = lax.all_to_all(
        slot_grad.reshape(experts, capacity), "expert", split_axis=0, concat_axis=0, tiled=True
    )
    grad_combine = returned.reshape(-1)[position].reshape(tok_rows, route_count)
    return (
        grad_weight[None],
        grad_gate.reshape(saved_gate.shape),
        grad_up.reshape(saved_up.shape),
        grad_combine,
    )


def solution(mesh):
    in_specs = (
        P(("expert", "dp"), None),
        P(("expert", "dp"), None),
        P(("expert", "dp"), None),
        P("expert", "dp", None, None, None),
        P("expert", "dp", None, None, None),
        P("expert", None, None),
    )
    out_specs = (
        P("expert", "dp", None),
        P("expert", "dp", None, None, None),
        P("expert", "dp", None, None, None),
        P(("expert", "dp"), None),
    )
    return jax.shard_map(local, mesh=mesh, in_specs=in_specs, out_specs=out_specs, check_vma=False)
```

```python
import jax
import jax.numpy as jnp
from jax import lax
from jax.sharding import PartitionSpec as P
from jax.experimental import pallas as pl
from jax.experimental.pallas import tpu as pltpu


def round_bf16(value):
    return lax.reduce_precision(value, exponent_bits=8, mantissa_bits=7)


def weight_pieces(weights):
    high = round_bf16(weights)
    rest = weights - high
    middle = round_bf16(rest)
    low = rest - middle
    return jnp.stack([high, middle, low], axis=-1).astype(jnp.bfloat16)


def partial_kernel(arrived_ref, gate_ref, up_ref, partial_ref, hidden_ref):
    features = partial_ref.shape[1]
    gate = gate_ref[...].astype(jnp.float32)
    sigmoid_gate = jax.nn.sigmoid(gate)
    hidden = (gate * sigmoid_gate * up_ref[...].astype(jnp.float32)).astype(jnp.bfloat16)
    hidden_ref[...] = hidden
    got = arrived_ref[:, features:features + 128].astype(jnp.float32)
    weights = (got[:, 0:1] + got[:, 1:2]) + got[:, 2:3]
    tile = 512 if features % 512 == 0 else features
    for start in range(0, features, tile):
        rows = arrived_ref[:, start:start + tile].astype(jnp.float32)
        weighted = (weights * rows).astype(jnp.bfloat16)
        partial_ref[:, start:start + tile] = lax.dot_general(
            hidden, weighted, (((0,), (0,)), ((), ())), preferred_element_type=jnp.float32
        ).astype(jnp.bfloat16)


def weighted_partial(arrived, gate, up, features):
    slots, hidden_count = gate.shape
    vmem = pl.BlockSpec(memory_space=pltpu.VMEM)
    flops = 2 * slots * hidden_count * features
    moved = 2 * (arrived.size + 2 * gate.size + hidden_count * features + gate.size)
    return pl.pallas_call(
        partial_kernel,
        out_shape=(
            jax.ShapeDtypeStruct((hidden_count, features), jnp.bfloat16),
            jax.ShapeDtypeStruct((slots, hidden_count), jnp.bfloat16),
        ),
        in_specs=[vmem, vmem, vmem],
        out_specs=(vmem, vmem),
        cost_estimate=pl.CostEstimate(
            flops=flops, bytes_accessed=moved, transcendentals=gate.size
        ),
    )(arrived, gate, up)


def local(out_grad, combine_weight, routes, saved_gate, saved_up, w_down):
    experts = lax.axis_size("expert")
    tok_rows, route_count = routes.shape
    capacity = saved_gate.shape[3]
    hidden_count = saved_gate.shape[4]
    feature_count = out_grad.shape[1]
    slots = experts * capacity
    lanes = 128

    flat_routes = routes.reshape(-1)
    route_total = flat_routes.shape[0]
    onehot = (flat_routes[:, None] == jnp.arange(experts, dtype=jnp.int32)[None, :]).astype(
        jnp.float32
    )
    order = jnp.arange(route_total, dtype=jnp.int32)
    earlier = (order[None, :] < order[:, None]).astype(jnp.bfloat16)
    before = jnp.dot(earlier, onehot.astype(jnp.bfloat16), preferred_element_type=jnp.float32)
    slot = jnp.sum(before * onehot, axis=1).astype(jnp.int32)
    position = flat_routes * capacity + slot

    slot_ids = jnp.arange(slots, dtype=jnp.int32)
    pick_route = position[None, :] == slot_ids[:, None]
    pick_token = pick_route.reshape(slots, tok_rows, route_count).any(axis=2)
    sent_rows = jnp.dot(
        pick_token.astype(out_grad.dtype), out_grad, preferred_element_type=jnp.float32
    ).astype(out_grad.dtype)
    pieces = weight_pieces(combine_weight.reshape(-1))
    pieces = jnp.pad(pieces, ((0, 0), (0, lanes - pieces.shape[1])))
    sent_pieces = jnp.dot(
        pick_route.astype(jnp.bfloat16), pieces, preferred_element_type=jnp.float32
    ).astype(jnp.bfloat16)
    packed = jnp.concatenate([sent_rows, sent_pieces], axis=1)
    arrived = lax.all_to_all(
        packed.reshape(experts, capacity, feature_count + lanes),
        "expert",
        split_axis=0,
        concat_axis=0,
        tiled=True,
    ).reshape(slots, feature_count + lanes)
    rows = arrived[:, :feature_count]
    got = arrived[:, feature_count:feature_count + 3].astype(jnp.float32)
    weights = (got[:, 0] + got[:, 1]) + got[:, 2]

    gate_bf = saved_gate.reshape(-1, hidden_count)
    up_bf = saved_up.reshape(-1, hidden_count)
    partial_grad, hidden = weighted_partial(arrived, gate_bf, up_bf, feature_count)
    summed = lax.psum_scatter(partial_grad, "dp", scatter_dimension=0, tiled=True)
    gate_pre = gate_bf.astype(jnp.float32)
    up_pre = up_bf.astype(jnp.float32)
    sigmoid_gate = jax.nn.sigmoid(gate_pre)
    grad_weight = summed.astype(jnp.float32)

    matrix = w_down[0]
    back = lax.dot_general(
        rows, matrix, (((1,), (1,)), ((), ())), preferred_element_type=jnp.float32
    )
    grad_hidden = weights[:, None] * back
    grad_gate = (
        grad_hidden * up_pre * sigmoid_gate * (1.0 + gate_pre * (1.0 - sigmoid_gate))
    ).astype(jnp.bfloat16)
    grad_up = (grad_hidden * gate_pre * sigmoid_gate).astype(jnp.bfloat16)
    slot_grad = jnp.sum(hidden.astype(jnp.float32) * back, axis=1)
    returned = lax.all_to_all(
        slot_grad.reshape(experts, capacity), "expert", split_axis=0, concat_axis=0, tiled=True
    )
    grad_combine = returned.reshape(-1)[position].reshape(tok_rows, route_count)
    return (
        grad_weight[None],
        grad_gate.reshape(saved_gate.shape),
        grad_up.reshape(saved_up.shape),
        grad_combine,
    )


def solution(mesh):
    in_specs = (
        P(("expert", "dp"), None),
        P(("expert", "dp"), None),
        P(("expert", "dp"), None),
        P("expert", "dp", None, None, None),
        P("expert", "dp", None, None, None),
        P("expert", None, None),
    )
    out_specs = (
        P("expert", "dp", None),
        P("expert", "dp", None, None, None),
        P("expert", "dp", None, None, None),
        P(("expert", "dp"), None),
    )
    return jax.shard_map(local, mesh=mesh, in_specs=in_specs, out_specs=out_specs, check_vma=False)
```

```python
import jax
import jax.numpy as jnp
from jax import lax
from jax.sharding import PartitionSpec as P
from jax.experimental import pallas as pl
from jax.experimental.pallas import tpu as pltpu


def round_bf16(value):
    return lax.reduce_precision(value, exponent_bits=8, mantissa_bits=7)


def weight_pieces(weights):
    high = round_bf16(weights)
    rest = weights - high
    middle = round_bf16(rest)
    low = rest - middle
    return jnp.stack([high, middle, low], axis=-1).astype(jnp.bfloat16)


def partial_kernel(arrived_ref, gate_ref, up_ref, partial_ref, hidden_ref):
    features = partial_ref.shape[1]
    gate = gate_ref[...].astype(jnp.float32)
    sigmoid_gate = 1.0 / (1.0 + jnp.exp(-gate))
    hidden = (gate * sigmoid_gate * up_ref[...].astype(jnp.float32)).astype(jnp.bfloat16)
    hidden_ref[...] = hidden
    hidden_t = jnp.transpose(hidden.astype(jnp.float32)).astype(jnp.bfloat16)
    got = arrived_ref[:, features:features + 128].astype(jnp.float32)
    weights = (got[:, 0:1] + got[:, 1:2]) + got[:, 2:3]
    tile = 512 if features % 512 == 0 else features
    for start in range(0, features, tile):
        rows = arrived_ref[:, start:start + tile].astype(jnp.float32)
        weighted = (weights * rows).astype(jnp.bfloat16)
        partial_ref[:, start:start + tile] = jnp.dot(
            hidden_t, weighted, preferred_element_type=jnp.float32
        ).astype(jnp.bfloat16)


def weighted_partial(arrived, gate, up, features):
    slots, hidden_count = gate.shape
    vmem = pl.BlockSpec(memory_space=pltpu.VMEM)
    flops = 2 * slots * hidden_count * features
    moved = 2 * (arrived.size + 2 * gate.size + hidden_count * features + gate.size)
    return pl.pallas_call(
        partial_kernel,
        out_shape=(
            jax.ShapeDtypeStruct((hidden_count, features), jnp.bfloat16),
            jax.ShapeDtypeStruct((slots, hidden_count), jnp.bfloat16),
        ),
        in_specs=[vmem, vmem, vmem],
        out_specs=(vmem, vmem),
        cost_estimate=pl.CostEstimate(
            flops=flops, bytes_accessed=moved, transcendentals=gate.size
        ),
    )(arrived, gate, up)


def local(out_grad, combine_weight, routes, saved_gate, saved_up, w_down):
    experts = lax.axis_size("expert")
    tok_rows, route_count = routes.shape
    capacity = saved_gate.shape[3]
    hidden_count = saved_gate.shape[4]
    feature_count = out_grad.shape[1]
    slots = experts * capacity
    lanes = 128

    by_route = routes.T
    expert_ids = jnp.arange(experts, dtype=jnp.int32)
    named = (by_route[:, None, :] == expert_ids[None, :, None]).astype(jnp.float32)
    per_token = jnp.sum(named, axis=0)
    token_ids = jnp.arange(tok_rows, dtype=jnp.int32)
    earlier = (token_ids[:, None] < token_ids[None, :]).astype(jnp.bfloat16)
    before = jnp.dot(
        per_token.astype(jnp.bfloat16), earlier, preferred_element_type=jnp.float32
    )
    slot = jnp.sum(named * before[None], axis=1).astype(jnp.int32)
    position = by_route * capacity + slot

    slot_ids = jnp.arange(slots, dtype=jnp.int32)
    pick_route = position.reshape(-1)[None, :] == slot_ids[:, None]
    pick_token = (position[0][None, :] == slot_ids[:, None]) | (
        position[1:][:, None, :] == slot_ids[None, :, None]
    ).any(axis=0)
    sent_rows = jnp.dot(
        pick_token.astype(out_grad.dtype), out_grad, preferred_element_type=jnp.float32
    ).astype(out_grad.dtype)
    pieces = weight_pieces(combine_weight.T.reshape(-1))
    pieces = jnp.pad(pieces, ((0, 0), (0, lanes - pieces.shape[1])))
    sent_pieces = jnp.dot(
        pick_route.astype(jnp.bfloat16), pieces, preferred_element_type=jnp.float32
    ).astype(jnp.bfloat16)
    packed = jnp.concatenate([sent_rows, sent_pieces], axis=1)
    arrived = lax.all_to_all(
        packed.reshape(experts, capacity, feature_count + lanes),
        "expert",
        split_axis=0,
        concat_axis=0,
        tiled=True,
    ).reshape(slots, feature_count + lanes)
    rows = arrived[:, :feature_count]
    got = arrived[:, feature_count:feature_count + 3].astype(jnp.float32)
    weights = (got[:, 0] + got[:, 1]) + got[:, 2]

    gate_bf = saved_gate.reshape(-1, hidden_count)
    up_bf = saved_up.reshape(-1, hidden_count)
    partial_grad, hidden = weighted_partial(arrived, gate_bf, up_bf, feature_count)
    summed = lax.psum_scatter(partial_grad, "dp", scatter_dimension=0, tiled=True)
    gate_pre = gate_bf.astype(jnp.float32)
    up_pre = up_bf.astype(jnp.float32)
    sigmoid_gate = jax.nn.sigmoid(gate_pre)
    grad_weight = summed.astype(jnp.float32)

    matrix = w_down[0]
    back = lax.dot_general(
        rows, matrix, (((1,), (1,)), ((), ())), preferred_element_type=jnp.float32
    )
    grad_hidden = weights[:, None] * back
    grad_gate = (
        grad_hidden * up_pre * sigmoid_gate * (1.0 + gate_pre * (1.0 - sigmoid_gate))
    ).astype(jnp.bfloat16)
    grad_up = (grad_hidden * gate_pre * sigmoid_gate).astype(jnp.bfloat16)
    slot_grad = jnp.sum(hidden.astype(jnp.float32) * back, axis=1)
    returned = lax.all_to_all(
        slot_grad.reshape(experts, capacity), "expert", split_axis=0, concat_axis=0, tiled=True
    )
    grad_combine = returned.reshape(-1)[position].T
    return (
        grad_weight[None],
        grad_gate.reshape(saved_gate.shape),
        grad_up.reshape(saved_up.shape),
        grad_combine,
    )


def solution(mesh):
    in_specs = (
        P(("expert", "dp"), None),
        P(("expert", "dp"), None),
        P(("expert", "dp"), None),
        P("expert", "dp", None, None, None),
        P("expert", "dp", None, None, None),
        P("expert", None, None),
    )
    out_specs = (
        P("expert", "dp", None),
        P("expert", "dp", None, None, None),
        P("expert", "dp", None, None, None),
        P(("expert", "dp"), None),
    )
    return jax.shard_map(local, mesh=mesh, in_specs=in_specs, out_specs=out_specs, check_vma=False)
```

```python
import functools

import jax
import jax.numpy as jnp
from jax import lax
from jax.sharding import PartitionSpec as P
from jax.experimental import pallas as pl
from jax.experimental.pallas import tpu as pltpu


def round_bf16(value):
    return lax.reduce_precision(value, exponent_bits=8, mantissa_bits=7)


def weight_pieces(weights):
    high = round_bf16(weights)
    rest = weights - high
    middle = round_bf16(rest)
    low = rest - middle
    return jnp.stack([high, middle, low], axis=-1).astype(jnp.bfloat16)


def front_kernel(routes_ref, weights_ref, rows_ref, packed_ref, position_ref, *, experts, capacity):
    route_count, tokens = routes_ref.shape
    slots, width = packed_ref.shape
    features = rows_ref.shape[1]
    padded = -(-experts // 8) * 8
    routes = routes_ref[...]
    expert_col = lax.broadcasted_iota(jnp.int32, (padded, tokens), 0)
    per_token = jnp.zeros((padded, tokens), jnp.float32)
    for k in range(route_count):
        per_token = per_token + jnp.where(routes[k:k + 1, :] == expert_col, 1.0, 0.0)
    earlier = jnp.where(
        lax.broadcasted_iota(jnp.int32, (tokens, tokens), 0)
        < lax.broadcasted_iota(jnp.int32, (tokens, tokens), 1), 1.0, 0.0
    ).astype(jnp.bfloat16)
    before = jnp.dot(per_token.astype(jnp.bfloat16), earlier, preferred_element_type=jnp.float32)
    slot_row = lax.broadcasted_iota(jnp.int32, (slots, tokens), 0)
    pick = jnp.zeros((slots, tokens), jnp.float32)
    weight = jnp.zeros((slots, 1), jnp.float32)
    for k in range(route_count):
        mine = routes[k:k + 1, :] == expert_col
        slot = jnp.sum(jnp.where(mine, before, 0.0), axis=0, keepdims=True).astype(jnp.int32)
        place = routes[k:k + 1, :] * capacity + slot
        position_ref[k:k + 1, :] = place
        chosen = slot_row == place
        pick = pick + jnp.where(chosen, 1.0, 0.0)
        weight = weight + jnp.sum(
            jnp.where(chosen, weights_ref[k:k + 1, :], 0.0), axis=1, keepdims=True
        )
    pick = pick.astype(jnp.bfloat16)
    tile = 512 if features % 512 == 0 else features
    for start in range(0, features, tile):
        packed_ref[:, start:start + tile] = jnp.dot(
            pick, rows_ref[:, start:start + tile], preferred_element_type=jnp.float32
        ).astype(jnp.bfloat16)
    high = weight.astype(jnp.bfloat16).astype(jnp.float32)
    rest = weight - high
    middle = rest.astype(jnp.bfloat16).astype(jnp.float32)
    low = rest - middle
    column = lax.broadcasted_iota(jnp.int32, (slots, width - features), 1)
    pieces = jnp.where(column == 0, high, jnp.where(column == 1, middle, jnp.where(column == 2, low, 0.0)))
    packed_ref[:, features:] = pieces.astype(jnp.bfloat16)


def pack_slots(routes_t, weights_t, rows, experts, capacity):
    route_count, tokens = routes_t.shape
    features = rows.shape[1]
    slots = experts * capacity
    vmem = pl.BlockSpec(memory_space=pltpu.VMEM)
    return pl.pallas_call(
        functools.partial(front_kernel, experts=experts, capacity=capacity),
        out_shape=(
            jax.ShapeDtypeStruct((slots, features + 128), jnp.bfloat16),
            jax.ShapeDtypeStruct((route_count, tokens), jnp.int32),
        ),
        in_specs=[vmem, vmem, vmem],
        out_specs=(vmem, vmem),
        cost_estimate=pl.CostEstimate(
            flops=2 * slots * tokens * features, bytes_accessed=2 * (rows.size + slots * features),
            transcendentals=0,
        ),
    )(routes_t, weights_t, rows)


def partial_kernel(arrived_ref, gate_ref, up_ref, partial_ref, hidden_ref):
    features = partial_ref.shape[1]
    gate = gate_ref[...].astype(jnp.float32)
    sigmoid_gate = 1.0 / (1.0 + jnp.exp(-gate))
    hidden = (gate * sigmoid_gate * up_ref[...].astype(jnp.float32)).astype(jnp.bfloat16)
    hidden_ref[...] = hidden
    hidden_t = jnp.transpose(hidden.astype(jnp.float32)).astype(jnp.bfloat16)
    got = arrived_ref[:, features:features + 128].astype(jnp.float32)
    weights = (got[:, 0:1] + got[:, 1:2]) + got[:, 2:3]
    tile = 512 if features % 512 == 0 else features
    for start in range(0, features, tile):
        rows = arrived_ref[:, start:start + tile].astype(jnp.float32)
        weighted = (weights * rows).astype(jnp.bfloat16)
        partial_ref[:, start:start + tile] = jnp.dot(
            hidden_t, weighted, preferred_element_type=jnp.float32
        ).astype(jnp.bfloat16)


def weighted_partial(arrived, gate, up, features):
    slots, hidden_count = gate.shape
    vmem = pl.BlockSpec(memory_space=pltpu.VMEM)
    flops = 2 * slots * hidden_count * features
    moved = 2 * (arrived.size + 2 * gate.size + hidden_count * features + gate.size)
    return pl.pallas_call(
        partial_kernel,
        out_shape=(
            jax.ShapeDtypeStruct((hidden_count, features), jnp.bfloat16),
            jax.ShapeDtypeStruct((slots, hidden_count), jnp.bfloat16),
        ),
        in_specs=[vmem, vmem, vmem],
        out_specs=(vmem, vmem),
        cost_estimate=pl.CostEstimate(
            flops=flops, bytes_accessed=moved, transcendentals=gate.size
        ),
    )(arrived, gate, up)


def local(out_grad, combine_weight, routes, saved_gate, saved_up, w_down):
    experts = lax.axis_size("expert")
    tok_rows, route_count = routes.shape
    capacity = saved_gate.shape[3]
    hidden_count = saved_gate.shape[4]
    feature_count = out_grad.shape[1]
    slots = experts * capacity
    lanes = 128

    packed, position = pack_slots(routes.T, combine_weight.T, out_grad, experts, capacity)
    arrived = lax.all_to_all(
        packed.reshape(experts, capacity, feature_count + lanes),
        "expert",
        split_axis=0,
        concat_axis=0,
        tiled=True,
    ).reshape(slots, feature_count + lanes)
    rows = arrived[:, :feature_count]
    got = arrived[:, feature_count:feature_count + 3].astype(jnp.float32)
    weights = (got[:, 0] + got[:, 1]) + got[:, 2]

    gate_bf = saved_gate.reshape(-1, hidden_count)
    up_bf = saved_up.reshape(-1, hidden_count)
    partial_grad, hidden = weighted_partial(arrived, gate_bf, up_bf, feature_count)
    summed = lax.psum_scatter(partial_grad, "dp", scatter_dimension=0, tiled=True)
    gate_pre = gate_bf.astype(jnp.float32)
    up_pre = up_bf.astype(jnp.float32)
    sigmoid_gate = jax.nn.sigmoid(gate_pre)
    grad_weight = summed.astype(jnp.float32)

    matrix = w_down[0]
    back = lax.dot_general(
        rows, matrix, (((1,), (1,)), ((), ())), preferred_element_type=jnp.float32
    )
    grad_hidden = weights[:, None] * back
    grad_gate = (
        grad_hidden * up_pre * sigmoid_gate * (1.0 + gate_pre * (1.0 - sigmoid_gate))
    ).astype(jnp.bfloat16)
    grad_up = (grad_hidden * gate_pre * sigmoid_gate).astype(jnp.bfloat16)
    slot_grad = jnp.sum(hidden.astype(jnp.float32) * back, axis=1)
    returned = lax.all_to_all(
        slot_grad.reshape(experts, capacity), "expert", split_axis=0, concat_axis=0, tiled=True
    )
    grad_combine = returned.reshape(-1)[position].T
    return (
        grad_weight[None],
        grad_gate.reshape(saved_gate.shape),
        grad_up.reshape(saved_up.shape),
        grad_combine,
    )


def solution(mesh):
    in_specs = (
        P(("expert", "dp"), None),
        P(("expert", "dp"), None),
        P(("expert", "dp"), None),
        P("expert", "dp", None, None, None),
        P("expert", "dp", None, None, None),
        P("expert", None, None),
    )
    out_specs = (
        P("expert", "dp", None),
        P("expert", "dp", None, None, None),
        P("expert", "dp", None, None, None),
        P(("expert", "dp"), None),
    )
    return jax.shard_map(local, mesh=mesh, in_specs=in_specs, out_specs=out_specs, check_vma=False)
```

```python
import functools

import jax
import jax.numpy as jnp
from jax import lax
from jax.sharding import PartitionSpec as P
from jax.experimental import pallas as pl
from jax.experimental.pallas import tpu as pltpu


def round_bf16(value):
    return lax.reduce_precision(value, exponent_bits=8, mantissa_bits=7)


def weight_pieces(weights):
    high = round_bf16(weights)
    rest = weights - high
    middle = round_bf16(rest)
    low = rest - middle
    return jnp.stack([high, middle, low], axis=-1).astype(jnp.bfloat16)


def front_kernel(routes_ref, weights_ref, rows_ref, packed_ref, position_ref, *, experts, capacity):
    route_count, tokens = routes_ref.shape
    slots, width = packed_ref.shape
    features = rows_ref.shape[1]
    padded = -(-experts // 8) * 8
    routes = routes_ref[...]
    expert_col = lax.broadcasted_iota(jnp.int32, (padded, tokens), 0)
    per_token = jnp.zeros((padded, tokens), jnp.float32)
    for k in range(route_count):
        per_token = per_token + jnp.where(routes[k:k + 1, :] == expert_col, 1.0, 0.0)
    earlier = jnp.where(
        lax.broadcasted_iota(jnp.int32, (tokens, tokens), 0)
        < lax.broadcasted_iota(jnp.int32, (tokens, tokens), 1), 1.0, 0.0
    ).astype(jnp.bfloat16)
    before = jnp.dot(per_token.astype(jnp.bfloat16), earlier, preferred_element_type=jnp.float32)
    slot_row = lax.broadcasted_iota(jnp.int32, (slots, tokens), 0)
    pick = jnp.zeros((slots, tokens), jnp.float32)
    weight = jnp.zeros((slots, 1), jnp.float32)
    for k in range(route_count):
        mine = routes[k:k + 1, :] == expert_col
        slot = jnp.sum(jnp.where(mine, before, 0.0), axis=0, keepdims=True).astype(jnp.int32)
        place = routes[k:k + 1, :] * capacity + slot
        position_ref[k:k + 1, :] = place
        chosen = slot_row == place
        pick = pick + jnp.where(chosen, 1.0, 0.0)
        weight = weight + jnp.sum(
            jnp.where(chosen, weights_ref[k:k + 1, :], 0.0), axis=1, keepdims=True
        )
    pick = pick.astype(jnp.bfloat16)
    tile = 512 if features % 512 == 0 else features
    for start in range(0, features, tile):
        packed_ref[:, start:start + tile] = jnp.dot(
            pick, rows_ref[:, start:start + tile], preferred_element_type=jnp.float32
        ).astype(jnp.bfloat16)
    high = weight.astype(jnp.bfloat16).astype(jnp.float32)
    rest = weight - high
    middle = rest.astype(jnp.bfloat16).astype(jnp.float32)
    low = rest - middle
    column = lax.broadcasted_iota(jnp.int32, (slots, width - features), 1)
    pieces = jnp.where(column == 0, high, jnp.where(column == 1, middle, jnp.where(column == 2, low, 0.0)))
    packed_ref[:, features:] = pieces.astype(jnp.bfloat16)


def pack_slots(routes_t, weights_t, rows, experts, capacity):
    route_count, tokens = routes_t.shape
    features = rows.shape[1]
    slots = experts * capacity
    vmem = pl.BlockSpec(memory_space=pltpu.VMEM)
    return pl.pallas_call(
        functools.partial(front_kernel, experts=experts, capacity=capacity),
        out_shape=(
            jax.ShapeDtypeStruct((slots, features + 128), jnp.bfloat16),
            jax.ShapeDtypeStruct((route_count, tokens), jnp.int32),
        ),
        in_specs=[vmem, vmem, vmem],
        out_specs=(vmem, vmem),
        cost_estimate=pl.CostEstimate(
            flops=2 * slots * tokens * features, bytes_accessed=2 * (rows.size + slots * features),
            transcendentals=0,
        ),
    )(routes_t, weights_t, rows)


def partial_kernel(arrived_hbm, gate_hbm, up_hbm, partial_hbm, hidden_hbm,
                   tiles_v, pieces_v, gate_v, up_v, hidden_v, out_v, in_sems, out_sems, *, tile):
    count = tiles_v.shape[0]
    features = count * tile
    lanes = pieces_v.shape[1]
    loads = [
        pltpu.make_async_copy(gate_hbm, gate_v, in_sems.at[0]),
        pltpu.make_async_copy(up_hbm, up_v, in_sems.at[1]),
        pltpu.make_async_copy(
            arrived_hbm.at[:, pl.ds(features, lanes)], pieces_v, in_sems.at[2]
        ),
    ]
    tiles = [
        pltpu.make_async_copy(
            arrived_hbm.at[:, pl.ds(part * tile, tile)], tiles_v.at[part], in_sems.at[3 + part]
        )
        for part in range(count)
    ]
    for copy in loads + tiles:
        copy.start()
    loads[0].wait()
    loads[1].wait()
    gate = gate_v[...].astype(jnp.float32)
    sigmoid_gate = 1.0 / (1.0 + jnp.exp(-gate))
    hidden = (gate * sigmoid_gate * up_v[...].astype(jnp.float32)).astype(jnp.bfloat16)
    hidden_v[...] = hidden
    store_hidden = pltpu.make_async_copy(hidden_v, hidden_hbm, out_sems.at[count])
    store_hidden.start()
    hidden_t = jnp.transpose(hidden.astype(jnp.float32)).astype(jnp.bfloat16)
    loads[2].wait()
    got = pieces_v[...].astype(jnp.float32)
    weights = (got[:, 0:1] + got[:, 1:2]) + got[:, 2:3]
    stores = []
    for part in range(count):
        tiles[part].wait()
        weighted = (weights * tiles_v[part].astype(jnp.float32)).astype(jnp.bfloat16)
        out_v[part] = jnp.dot(hidden_t, weighted, preferred_element_type=jnp.float32).astype(
            jnp.bfloat16
        )
        store = pltpu.make_async_copy(
            out_v.at[part], partial_hbm.at[:, pl.ds(part * tile, tile)], out_sems.at[part]
        )
        store.start()
        stores.append(store)
    for store in stores:
        store.wait()
    store_hidden.wait()


def weighted_partial(arrived, gate, up, features):
    slots, hidden_count = gate.shape
    lanes = arrived.shape[1] - features
    tile = 512 if features % 512 == 0 else features
    count = features // tile
    flops = 2 * slots * hidden_count * features
    moved = 2 * (arrived.size + 2 * gate.size + hidden_count * features + gate.size)
    anywhere = pl.BlockSpec(memory_space=pl.ANY)
    return pl.pallas_call(
        functools.partial(partial_kernel, tile=tile),
        out_shape=(
            jax.ShapeDtypeStruct((hidden_count, features), jnp.bfloat16),
            jax.ShapeDtypeStruct((slots, hidden_count), jnp.bfloat16),
        ),
        in_specs=[anywhere, anywhere, anywhere],
        out_specs=(anywhere, anywhere),
        scratch_shapes=[
            pltpu.VMEM((count, slots, tile), jnp.bfloat16),
            pltpu.VMEM((slots, lanes), jnp.bfloat16),
            pltpu.VMEM((slots, hidden_count), jnp.bfloat16),
            pltpu.VMEM((slots, hidden_count), jnp.bfloat16),
            pltpu.VMEM((slots, hidden_count), jnp.bfloat16),
            pltpu.VMEM((count, hidden_count, tile), jnp.bfloat16),
            pltpu.SemaphoreType.DMA((3 + count,)),
            pltpu.SemaphoreType.DMA((count + 1,)),
        ],
        cost_estimate=pl.CostEstimate(
            flops=flops, bytes_accessed=moved, transcendentals=gate.size
        ),
    )(arrived, gate, up)


def local(out_grad, combine_weight, routes, saved_gate, saved_up, w_down):
    experts = lax.axis_size("expert")
    tok_rows, route_count = routes.shape
    capacity = saved_gate.shape[3]
    hidden_count = saved_gate.shape[4]
    feature_count = out_grad.shape[1]
    slots = experts * capacity
    lanes = 128

    packed, position = pack_slots(routes.T, combine_weight.T, out_grad, experts, capacity)
    arrived = lax.all_to_all(
        packed.reshape(experts, capacity, feature_count + lanes),
        "expert",
        split_axis=0,
        concat_axis=0,
        tiled=True,
    ).reshape(slots, feature_count + lanes)
    rows = arrived[:, :feature_count]
    got = arrived[:, feature_count:feature_count + 3].astype(jnp.float32)
    weights = (got[:, 0] + got[:, 1]) + got[:, 2]

    gate_bf = saved_gate.reshape(-1, hidden_count)
    up_bf = saved_up.reshape(-1, hidden_count)
    partial_grad, hidden = weighted_partial(arrived, gate_bf, up_bf, feature_count)
    summed = lax.psum_scatter(partial_grad, "dp", scatter_dimension=0, tiled=True)
    gate_pre = gate_bf.astype(jnp.float32)
    up_pre = up_bf.astype(jnp.float32)
    sigmoid_gate = jax.nn.sigmoid(gate_pre)
    grad_weight = summed.astype(jnp.float32)

    matrix = w_down[0]
    back = lax.dot_general(
        rows, matrix, (((1,), (1,)), ((), ())), preferred_element_type=jnp.float32
    )
    grad_hidden = weights[:, None] * back
    grad_gate = (
        grad_hidden * up_pre * sigmoid_gate * (1.0 + gate_pre * (1.0 - sigmoid_gate))
    ).astype(jnp.bfloat16)
    grad_up = (grad_hidden * gate_pre * sigmoid_gate).astype(jnp.bfloat16)
    slot_grad = jnp.sum(hidden.astype(jnp.float32) * back, axis=1)
    returned = lax.all_to_all(
        slot_grad.reshape(experts, capacity), "expert", split_axis=0, concat_axis=0, tiled=True
    )
    grad_combine = returned.reshape(-1)[position].T
    return (
        grad_weight[None],
        grad_gate.reshape(saved_gate.shape),
        grad_up.reshape(saved_up.shape),
        grad_combine,
    )


def solution(mesh):
    in_specs = (
        P(("expert", "dp"), None),
        P(("expert", "dp"), None),
        P(("expert", "dp"), None),
        P("expert", "dp", None, None, None),
        P("expert", "dp", None, None, None),
        P("expert", None, None),
    )
    out_specs = (
        P("expert", "dp", None),
        P("expert", "dp", None, None, None),
        P("expert", "dp", None, None, None),
        P(("expert", "dp"), None),
    )
    return jax.shard_map(local, mesh=mesh, in_specs=in_specs, out_specs=out_specs, check_vma=False)
```

```python
import functools

import jax
import jax.numpy as jnp
from jax import lax
from jax.sharding import PartitionSpec as P
from jax.experimental import pallas as pl
from jax.experimental.pallas import tpu as pltpu


def round_bf16(value):
    return lax.reduce_precision(value, exponent_bits=8, mantissa_bits=7)


def weight_pieces(weights):
    high = round_bf16(weights)
    rest = weights - high
    middle = round_bf16(rest)
    low = rest - middle
    return jnp.stack([high, middle, low], axis=-1).astype(jnp.bfloat16)


def front_kernel(routes_ref, weights_ref, rows_ref, packed_ref, position_ref, *, experts, capacity):
    route_count, tokens = routes_ref.shape
    slots, width = packed_ref.shape
    features = rows_ref.shape[1]
    padded = -(-experts // 8) * 8
    routes = routes_ref[...]
    expert_col = lax.broadcasted_iota(jnp.int32, (padded, tokens), 0)
    per_token = jnp.zeros((padded, tokens), jnp.float32)
    for k in range(route_count):
        per_token = per_token + jnp.where(routes[k:k + 1, :] == expert_col, 1.0, 0.0)
    earlier = jnp.where(
        lax.broadcasted_iota(jnp.int32, (tokens, tokens), 0)
        < lax.broadcasted_iota(jnp.int32, (tokens, tokens), 1), 1.0, 0.0
    ).astype(jnp.bfloat16)
    before = jnp.dot(per_token.astype(jnp.bfloat16), earlier, preferred_element_type=jnp.float32)
    slot_row = lax.broadcasted_iota(jnp.int32, (slots, tokens), 0)
    pick = jnp.zeros((slots, tokens), jnp.float32)
    weight = jnp.zeros((slots, 1), jnp.float32)
    for k in range(route_count):
        mine = routes[k:k + 1, :] == expert_col
        slot = jnp.sum(jnp.where(mine, before, 0.0), axis=0, keepdims=True).astype(jnp.int32)
        place = routes[k:k + 1, :] * capacity + slot
        position_ref[k:k + 1, :] = place
        chosen = slot_row == place
        pick = pick + jnp.where(chosen, 1.0, 0.0)
        weight = weight + jnp.sum(
            jnp.where(chosen, weights_ref[k:k + 1, :], 0.0), axis=1, keepdims=True
        )
    pick = pick.astype(jnp.bfloat16)
    tile = 512 if features % 512 == 0 else features
    for start in range(0, features, tile):
        packed_ref[:, start:start + tile] = jnp.dot(
            pick, rows_ref[:, start:start + tile], preferred_element_type=jnp.float32
        ).astype(jnp.bfloat16)
    high = weight.astype(jnp.bfloat16).astype(jnp.float32)
    rest = weight - high
    middle = rest.astype(jnp.bfloat16).astype(jnp.float32)
    low = rest - middle
    column = lax.broadcasted_iota(jnp.int32, (slots, width - features), 1)
    pieces = jnp.where(column == 0, high, jnp.where(column == 1, middle, jnp.where(column == 2, low, 0.0)))
    packed_ref[:, features:] = pieces.astype(jnp.bfloat16)


def pack_slots(routes_t, weights_t, rows, experts, capacity):
    route_count, tokens = routes_t.shape
    features = rows.shape[1]
    slots = experts * capacity
    vmem = pl.BlockSpec(memory_space=pltpu.VMEM)
    return pl.pallas_call(
        functools.partial(front_kernel, experts=experts, capacity=capacity),
        out_shape=(
            jax.ShapeDtypeStruct((slots, features + 128), jnp.bfloat16),
            jax.ShapeDtypeStruct((route_count, tokens), jnp.int32),
        ),
        in_specs=[vmem, vmem, vmem],
        out_specs=(vmem, vmem),
        cost_estimate=pl.CostEstimate(
            flops=2 * slots * tokens * features, bytes_accessed=2 * (rows.size + slots * features),
            transcendentals=0,
        ),
    )(routes_t, weights_t, rows)


def hidden_kernel(gate_ref, up_ref, hidden_ref, hidden_t_ref):
    gate = gate_ref[...].astype(jnp.float32)
    sigmoid_gate = 1.0 / (1.0 + jnp.exp(-gate))
    hidden = (gate * sigmoid_gate * up_ref[...].astype(jnp.float32)).astype(jnp.bfloat16)
    hidden_ref[...] = hidden
    hidden_t_ref[...] = jnp.transpose(hidden.astype(jnp.float32)).astype(jnp.bfloat16)


def hidden_pair(gate, up):
    slots, hidden_count = gate.shape
    vmem = pl.BlockSpec(memory_space=pltpu.VMEM)
    return pl.pallas_call(
        hidden_kernel,
        out_shape=(
            jax.ShapeDtypeStruct((slots, hidden_count), jnp.bfloat16),
            jax.ShapeDtypeStruct((hidden_count, slots), jnp.bfloat16),
        ),
        in_specs=[vmem, vmem],
        out_specs=(vmem, vmem),
        cost_estimate=pl.CostEstimate(
            flops=8 * gate.size, bytes_accessed=8 * gate.size, transcendentals=gate.size
        ),
    )(gate, up)


def partial_kernel(arrived_hbm, hidden_t_hbm, partial_hbm, tiles_v, pieces_v, hidden_t_v,
                   out_v, in_sems, out_sems, *, tile):
    count = tiles_v.shape[0]
    features = count * tile
    lanes = pieces_v.shape[1]
    loads = [
        pltpu.make_async_copy(hidden_t_hbm, hidden_t_v, in_sems.at[0]),
        pltpu.make_async_copy(
            arrived_hbm.at[:, pl.ds(features, lanes)], pieces_v, in_sems.at[1]
        ),
    ]
    tiles = [
        pltpu.make_async_copy(
            arrived_hbm.at[:, pl.ds(part * tile, tile)], tiles_v.at[part], in_sems.at[2 + part]
        )
        for part in range(count)
    ]
    for copy in loads + tiles:
        copy.start()
    loads[1].wait()
    got = pieces_v[...].astype(jnp.float32)
    weights = (got[:, 0:1] + got[:, 1:2]) + got[:, 2:3]
    loads[0].wait()
    stores = []
    for part in range(count):
        tiles[part].wait()
        weighted = (weights * tiles_v[part].astype(jnp.float32)).astype(jnp.bfloat16)
        out_v[part] = jnp.dot(
            hidden_t_v[...], weighted, preferred_element_type=jnp.float32
        ).astype(jnp.bfloat16)
        store = pltpu.make_async_copy(
            out_v.at[part], partial_hbm.at[:, pl.ds(part * tile, tile)], out_sems.at[part]
        )
        store.start()
        stores.append(store)
    for store in stores:
        store.wait()


def weighted_partial(arrived, hidden_t, features):
    hidden_count, slots = hidden_t.shape
    lanes = arrived.shape[1] - features
    tile = 512 if features % 512 == 0 else features
    count = features // tile
    flops = 2 * slots * hidden_count * features
    moved = 2 * (arrived.size + hidden_t.size + hidden_count * features)
    anywhere = pl.BlockSpec(memory_space=pl.ANY)
    return pl.pallas_call(
        functools.partial(partial_kernel, tile=tile),
        out_shape=jax.ShapeDtypeStruct((hidden_count, features), jnp.bfloat16),
        in_specs=[anywhere, anywhere],
        out_specs=anywhere,
        scratch_shapes=[
            pltpu.VMEM((count, slots, tile), jnp.bfloat16),
            pltpu.VMEM((slots, lanes), jnp.bfloat16),
            pltpu.VMEM((hidden_count, slots), jnp.bfloat16),
            pltpu.VMEM((count, hidden_count, tile), jnp.bfloat16),
            pltpu.SemaphoreType.DMA((2 + count,)),
            pltpu.SemaphoreType.DMA((count,)),
        ],
        cost_estimate=pl.CostEstimate(flops=flops, bytes_accessed=moved, transcendentals=0),
    )(arrived, hidden_t)


def local(out_grad, combine_weight, routes, saved_gate, saved_up, w_down):
    experts = lax.axis_size("expert")
    tok_rows, route_count = routes.shape
    capacity = saved_gate.shape[3]
    hidden_count = saved_gate.shape[4]
    feature_count = out_grad.shape[1]
    slots = experts * capacity
    lanes = 128

    packed, position = pack_slots(routes.T, combine_weight.T, out_grad, experts, capacity)
    arrived = lax.all_to_all(
        packed.reshape(experts, capacity, feature_count + lanes),
        "expert",
        split_axis=0,
        concat_axis=0,
        tiled=True,
    ).reshape(slots, feature_count + lanes)
    rows = arrived[:, :feature_count]
    got = arrived[:, feature_count:feature_count + 3].astype(jnp.float32)
    weights = (got[:, 0] + got[:, 1]) + got[:, 2]

    gate_bf = saved_gate.reshape(-1, hidden_count)
    up_bf = saved_up.reshape(-1, hidden_count)
    hidden, hidden_t = hidden_pair(gate_bf, up_bf)
    partial_grad = weighted_partial(arrived, hidden_t, feature_count)
    summed = lax.psum_scatter(partial_grad, "dp", scatter_dimension=0, tiled=True)
    gate_pre = gate_bf.astype(jnp.float32)
    up_pre = up_bf.astype(jnp.float32)
    sigmoid_gate = jax.nn.sigmoid(gate_pre)
    grad_weight = summed.astype(jnp.float32)

    matrix = w_down[0]
    back = lax.dot_general(
        rows, matrix, (((1,), (1,)), ((), ())), preferred_element_type=jnp.float32
    )
    grad_hidden = weights[:, None] * back
    grad_gate = (
        grad_hidden * up_pre * sigmoid_gate * (1.0 + gate_pre * (1.0 - sigmoid_gate))
    ).astype(jnp.bfloat16)
    grad_up = (grad_hidden * gate_pre * sigmoid_gate).astype(jnp.bfloat16)
    slot_grad = jnp.sum(hidden.astype(jnp.float32) * back, axis=1)
    returned = lax.all_to_all(
        slot_grad.reshape(experts, capacity), "expert", split_axis=0, concat_axis=0, tiled=True
    )
    grad_combine = returned.reshape(-1)[position].T
    return (
        grad_weight[None],
        grad_gate.reshape(saved_gate.shape),
        grad_up.reshape(saved_up.shape),
        grad_combine,
    )


def solution(mesh):
    in_specs = (
        P(("expert", "dp"), None),
        P(("expert", "dp"), None),
        P(("expert", "dp"), None),
        P("expert", "dp", None, None, None),
        P("expert", "dp", None, None, None),
        P("expert", None, None),
    )
    out_specs = (
        P("expert", "dp", None),
        P("expert", "dp", None, None, None),
        P("expert", "dp", None, None, None),
        P(("expert", "dp"), None),
    )
    return jax.shard_map(local, mesh=mesh, in_specs=in_specs, out_specs=out_specs, check_vma=False)
```

```python
import functools

import jax
import jax.numpy as jnp
from jax import lax
from jax.sharding import PartitionSpec as P
from jax.experimental import pallas as pl
from jax.experimental.pallas import tpu as pltpu


def round_bf16(value):
    return lax.reduce_precision(value, exponent_bits=8, mantissa_bits=7)


def weight_pieces(weights):
    high = round_bf16(weights)
    rest = weights - high
    middle = round_bf16(rest)
    low = rest - middle
    return jnp.stack([high, middle, low], axis=-1).astype(jnp.bfloat16)


def front_kernel(routes_ref, weights_ref, rows_ref, packed_ref, position_ref, *, experts, capacity):
    route_count, tokens = routes_ref.shape
    slots, width = packed_ref.shape
    features = rows_ref.shape[1]
    padded = -(-experts // 8) * 8
    routes = routes_ref[...]
    expert_col = lax.broadcasted_iota(jnp.int32, (padded, tokens), 0)
    per_token = jnp.zeros((padded, tokens), jnp.float32)
    for k in range(route_count):
        per_token = per_token + jnp.where(routes[k:k + 1, :] == expert_col, 1.0, 0.0)
    earlier = jnp.where(
        lax.broadcasted_iota(jnp.int32, (tokens, tokens), 0)
        < lax.broadcasted_iota(jnp.int32, (tokens, tokens), 1), 1.0, 0.0
    ).astype(jnp.bfloat16)
    before = jnp.dot(per_token.astype(jnp.bfloat16), earlier, preferred_element_type=jnp.float32)
    slot_row = lax.broadcasted_iota(jnp.int32, (slots, tokens), 0)
    pick = jnp.zeros((slots, tokens), jnp.float32)
    weight = jnp.zeros((slots, 1), jnp.float32)
    for k in range(route_count):
        mine = routes[k:k + 1, :] == expert_col
        slot = jnp.sum(jnp.where(mine, before, 0.0), axis=0, keepdims=True).astype(jnp.int32)
        place = routes[k:k + 1, :] * capacity + slot
        position_ref[k:k + 1, :] = place
        chosen = slot_row == place
        pick = pick + jnp.where(chosen, 1.0, 0.0)
        weight = weight + jnp.sum(
            jnp.where(chosen, weights_ref[k:k + 1, :], 0.0), axis=1, keepdims=True
        )
    pick = pick.astype(jnp.bfloat16)
    tile = 512 if features % 512 == 0 else features
    for start in range(0, features, tile):
        packed_ref[:, start:start + tile] = jnp.dot(
            pick, rows_ref[:, start:start + tile], preferred_element_type=jnp.float32
        ).astype(jnp.bfloat16)
    high = weight.astype(jnp.bfloat16).astype(jnp.float32)
    rest = weight - high
    middle = rest.astype(jnp.bfloat16).astype(jnp.float32)
    low = rest - middle
    column = lax.broadcasted_iota(jnp.int32, (slots, width - features), 1)
    pieces = jnp.where(column == 0, high, jnp.where(column == 1, middle, jnp.where(column == 2, low, 0.0)))
    packed_ref[:, features:] = pieces.astype(jnp.bfloat16)


def pack_slots(routes_t, weights_t, rows, experts, capacity):
    route_count, tokens = routes_t.shape
    features = rows.shape[1]
    slots = experts * capacity
    vmem = pl.BlockSpec(memory_space=pltpu.VMEM)
    return pl.pallas_call(
        functools.partial(front_kernel, experts=experts, capacity=capacity),
        out_shape=(
            jax.ShapeDtypeStruct((slots, features + 128), jnp.bfloat16),
            jax.ShapeDtypeStruct((route_count, tokens), jnp.int32),
        ),
        in_specs=[vmem, vmem, vmem],
        out_specs=(vmem, vmem),
        cost_estimate=pl.CostEstimate(
            flops=2 * slots * tokens * features, bytes_accessed=2 * (rows.size + slots * features),
            transcendentals=0,
        ),
    )(routes_t, weights_t, rows)


def hidden_kernel(gate_ref, up_ref, hidden_ref, hidden_t_ref):
    gate = gate_ref[...].astype(jnp.float32)
    sigmoid_gate = 1.0 / (1.0 + jnp.exp(-gate))
    hidden = (gate * sigmoid_gate * up_ref[...].astype(jnp.float32)).astype(jnp.bfloat16)
    hidden_ref[...] = hidden
    hidden_t_ref[...] = jnp.transpose(hidden.astype(jnp.float32)).astype(jnp.bfloat16)


def hidden_pair(gate, up):
    slots, hidden_count = gate.shape
    vmem = pl.BlockSpec(memory_space=pltpu.VMEM)
    return pl.pallas_call(
        hidden_kernel,
        out_shape=(
            jax.ShapeDtypeStruct((slots, hidden_count), jnp.bfloat16),
            jax.ShapeDtypeStruct((hidden_count, slots), jnp.bfloat16),
        ),
        in_specs=[vmem, vmem],
        out_specs=(vmem, vmem),
        cost_estimate=pl.CostEstimate(
            flops=8 * gate.size, bytes_accessed=8 * gate.size, transcendentals=gate.size
        ),
    )(gate, up)


def partial_kernel(arrived_hbm, hidden_t_hbm, partial_hbm, tiles_v, pieces_v, hidden_t_v,
                   out_v, in_sems, out_sems, *, tile):
    count = tiles_v.shape[0]
    features = count * tile
    lanes = pieces_v.shape[1]
    loads = [
        pltpu.make_async_copy(hidden_t_hbm, hidden_t_v, in_sems.at[0]),
        pltpu.make_async_copy(
            arrived_hbm.at[:, pl.ds(features, lanes)], pieces_v, in_sems.at[1]
        ),
    ]
    tiles = [
        pltpu.make_async_copy(
            arrived_hbm.at[:, pl.ds(part * tile, tile)], tiles_v.at[part], in_sems.at[2 + part]
        )
        for part in range(count)
    ]
    for copy in loads + tiles:
        copy.start()
    loads[1].wait()
    got = jnp.transpose(pieces_v[...].astype(jnp.float32))
    weights = (got[0:1, :] + got[1:2, :]) + got[2:3, :]
    loads[0].wait()
    scaled = (hidden_t_v[...].astype(jnp.float32) * weights).astype(jnp.bfloat16)
    stores = []
    for part in range(count):
        tiles[part].wait()
        out_v[part] = jnp.dot(
            scaled, tiles_v[part], preferred_element_type=jnp.float32
        ).astype(jnp.bfloat16)
        store = pltpu.make_async_copy(
            out_v.at[part], partial_hbm.at[:, pl.ds(part * tile, tile)], out_sems.at[part]
        )
        store.start()
        stores.append(store)
    for store in stores:
        store.wait()


def weighted_partial(arrived, hidden_t, features):
    hidden_count, slots = hidden_t.shape
    lanes = arrived.shape[1] - features
    tile = 512 if features % 512 == 0 else features
    count = features // tile
    flops = 2 * slots * hidden_count * features
    moved = 2 * (arrived.size + hidden_t.size + hidden_count * features)
    anywhere = pl.BlockSpec(memory_space=pl.ANY)
    return pl.pallas_call(
        functools.partial(partial_kernel, tile=tile),
        out_shape=jax.ShapeDtypeStruct((hidden_count, features), jnp.bfloat16),
        in_specs=[anywhere, anywhere],
        out_specs=anywhere,
        scratch_shapes=[
            pltpu.VMEM((count, slots, tile), jnp.bfloat16),
            pltpu.VMEM((slots, lanes), jnp.bfloat16),
            pltpu.VMEM((hidden_count, slots), jnp.bfloat16),
            pltpu.VMEM((count, hidden_count, tile), jnp.bfloat16),
            pltpu.SemaphoreType.DMA((2 + count,)),
            pltpu.SemaphoreType.DMA((count,)),
        ],
        cost_estimate=pl.CostEstimate(flops=flops, bytes_accessed=moved, transcendentals=0),
    )(arrived, hidden_t)


def local(out_grad, combine_weight, routes, saved_gate, saved_up, w_down):
    experts = lax.axis_size("expert")
    tok_rows, route_count = routes.shape
    capacity = saved_gate.shape[3]
    hidden_count = saved_gate.shape[4]
    feature_count = out_grad.shape[1]
    slots = experts * capacity
    lanes = 128

    packed, position = pack_slots(routes.T, combine_weight.T, out_grad, experts, capacity)
    arrived = lax.all_to_all(
        packed.reshape(experts, capacity, feature_count + lanes),
        "expert",
        split_axis=0,
        concat_axis=0,
        tiled=True,
    ).reshape(slots, feature_count + lanes)
    rows = arrived[:, :feature_count]
    got = arrived[:, feature_count:feature_count + 3].astype(jnp.float32)
    weights = (got[:, 0] + got[:, 1]) + got[:, 2]

    gate_bf = saved_gate.reshape(-1, hidden_count)
    up_bf = saved_up.reshape(-1, hidden_count)
    hidden, hidden_t = hidden_pair(gate_bf, up_bf)
    partial_grad = weighted_partial(arrived, hidden_t, feature_count)
    summed = lax.psum_scatter(partial_grad, "dp", scatter_dimension=0, tiled=True)
    gate_pre = gate_bf.astype(jnp.float32)
    up_pre = up_bf.astype(jnp.float32)
    sigmoid_gate = jax.nn.sigmoid(gate_pre)
    grad_weight = summed.astype(jnp.float32)

    matrix = w_down[0]
    back = lax.dot_general(
        rows, matrix, (((1,), (1,)), ((), ())), preferred_element_type=jnp.float32
    )
    grad_hidden = weights[:, None] * back
    grad_gate = (
        grad_hidden * up_pre * sigmoid_gate * (1.0 + gate_pre * (1.0 - sigmoid_gate))
    ).astype(jnp.bfloat16)
    grad_up = (grad_hidden * gate_pre * sigmoid_gate).astype(jnp.bfloat16)
    slot_grad = jnp.sum(hidden.astype(jnp.float32) * back, axis=1)
    returned = lax.all_to_all(
        slot_grad.reshape(experts, capacity), "expert", split_axis=0, concat_axis=0, tiled=True
    )
    grad_combine = returned.reshape(-1)[position].T
    return (
        grad_weight[None],
        grad_gate.reshape(saved_gate.shape),
        grad_up.reshape(saved_up.shape),
        grad_combine,
    )


def solution(mesh):
    in_specs = (
        P(("expert", "dp"), None),
        P(("expert", "dp"), None),
        P(("expert", "dp"), None),
        P("expert", "dp", None, None, None),
        P("expert", "dp", None, None, None),
        P("expert", None, None),
    )
    out_specs = (
        P("expert", "dp", None),
        P("expert", "dp", None, None, None),
        P("expert", "dp", None, None, None),
        P(("expert", "dp"), None),
    )
    return jax.shard_map(local, mesh=mesh, in_specs=in_specs, out_specs=out_specs, check_vma=False)
```

```python
import functools

import jax
import jax.numpy as jnp
from jax import lax
from jax.sharding import PartitionSpec as P
from jax.experimental import pallas as pl
from jax.experimental.pallas import tpu as pltpu


def round_bf16(value):
    return lax.reduce_precision(value, exponent_bits=8, mantissa_bits=7)


def weight_pieces(weights):
    high = round_bf16(weights)
    rest = weights - high
    middle = round_bf16(rest)
    low = rest - middle
    return jnp.stack([high, middle, low], axis=-1).astype(jnp.bfloat16)


def front_kernel(routes_ref, weights_ref, rows_ref, packed_hbm, position_ref, packed_v, sems, *,
                 experts, capacity):
    route_count, tokens = routes_ref.shape
    slots, width = packed_v.shape
    features = rows_ref.shape[1]
    padded = -(-experts // 8) * 8
    routes = routes_ref[...]
    expert_col = lax.broadcasted_iota(jnp.int32, (padded, tokens), 0)
    per_token = jnp.zeros((padded, tokens), jnp.float32)
    for k in range(route_count):
        per_token = per_token + jnp.where(routes[k:k + 1, :] == expert_col, 1.0, 0.0)
    earlier = jnp.where(
        lax.broadcasted_iota(jnp.int32, (tokens, tokens), 0)
        < lax.broadcasted_iota(jnp.int32, (tokens, tokens), 1), 1.0, 0.0
    ).astype(jnp.bfloat16)
    before = jnp.dot(per_token.astype(jnp.bfloat16), earlier, preferred_element_type=jnp.float32)
    slot_row = lax.broadcasted_iota(jnp.int32, (slots, tokens), 0)
    pick = jnp.zeros((slots, tokens), jnp.float32)
    weight = jnp.zeros((slots, 1), jnp.float32)
    for k in range(route_count):
        mine = routes[k:k + 1, :] == expert_col
        slot = jnp.sum(jnp.where(mine, before, 0.0), axis=0, keepdims=True).astype(jnp.int32)
        place = routes[k:k + 1, :] * capacity + slot
        position_ref[k:k + 1, :] = place
        chosen = slot_row == place
        pick = pick + jnp.where(chosen, 1.0, 0.0)
        weight = weight + jnp.sum(
            jnp.where(chosen, weights_ref[k:k + 1, :], 0.0), axis=1, keepdims=True
        )
    pick = pick.astype(jnp.bfloat16)
    tile = 512 if features % 512 == 0 else features
    stores = []
    for part, start in enumerate(range(0, features, tile)):
        packed_v[:, start:start + tile] = jnp.dot(
            pick, rows_ref[:, start:start + tile], preferred_element_type=jnp.float32
        ).astype(jnp.bfloat16)
        store = pltpu.make_async_copy(
            packed_v.at[:, pl.ds(start, tile)], packed_hbm.at[:, pl.ds(start, tile)],
            sems.at[part],
        )
        store.start()
        stores.append(store)
    high = weight.astype(jnp.bfloat16).astype(jnp.float32)
    rest = weight - high
    middle = rest.astype(jnp.bfloat16).astype(jnp.float32)
    low = rest - middle
    column = lax.broadcasted_iota(jnp.int32, (slots, width - features), 1)
    pieces = jnp.where(column == 0, high, jnp.where(column == 1, middle, jnp.where(column == 2, low, 0.0)))
    packed_v[:, features:] = pieces.astype(jnp.bfloat16)
    store = pltpu.make_async_copy(
        packed_v.at[:, pl.ds(features, width - features)],
        packed_hbm.at[:, pl.ds(features, width - features)],
        sems.at[len(stores)],
    )
    store.start()
    stores.append(store)
    for store in stores:
        store.wait()


def pack_slots(routes_t, weights_t, rows, experts, capacity):
    route_count, tokens = routes_t.shape
    features = rows.shape[1]
    slots = experts * capacity
    vmem = pl.BlockSpec(memory_space=pltpu.VMEM)
    return pl.pallas_call(
        functools.partial(front_kernel, experts=experts, capacity=capacity),
        out_shape=(
            jax.ShapeDtypeStruct((slots, features + 128), jnp.bfloat16),
            jax.ShapeDtypeStruct((route_count, tokens), jnp.int32),
        ),
        in_specs=[vmem, vmem, vmem],
        out_specs=(pl.BlockSpec(memory_space=pl.ANY), vmem),
        scratch_shapes=[
            pltpu.VMEM((slots, features + 128), jnp.bfloat16),
            pltpu.SemaphoreType.DMA((features // (512 if features % 512 == 0 else features) + 1,)),
        ],
        cost_estimate=pl.CostEstimate(
            flops=2 * slots * tokens * features, bytes_accessed=2 * (rows.size + slots * features),
            transcendentals=0,
        ),
    )(routes_t, weights_t, rows)


def hidden_kernel(gate_ref, up_ref, hidden_ref, hidden_t_ref):
    gate = gate_ref[...].astype(jnp.float32)
    sigmoid_gate = 1.0 / (1.0 + jnp.exp(-gate))
    hidden = (gate * sigmoid_gate * up_ref[...].astype(jnp.float32)).astype(jnp.bfloat16)
    hidden_ref[...] = hidden
    hidden_t_ref[...] = jnp.transpose(hidden.astype(jnp.float32)).astype(jnp.bfloat16)


def hidden_pair(gate, up):
    slots, hidden_count = gate.shape
    vmem = pl.BlockSpec(memory_space=pltpu.VMEM)
    return pl.pallas_call(
        hidden_kernel,
        out_shape=(
            jax.ShapeDtypeStruct((slots, hidden_count), jnp.bfloat16),
            jax.ShapeDtypeStruct((hidden_count, slots), jnp.bfloat16),
        ),
        in_specs=[vmem, vmem],
        out_specs=(vmem, vmem),
        cost_estimate=pl.CostEstimate(
            flops=8 * gate.size, bytes_accessed=8 * gate.size, transcendentals=gate.size
        ),
    )(gate, up)


def partial_kernel(arrived_hbm, hidden_t_hbm, partial_hbm, tiles_v, pieces_v, hidden_t_v,
                   out_v, in_sems, out_sems, *, tile):
    count = tiles_v.shape[0]
    features = count * tile
    lanes = pieces_v.shape[1]
    loads = [
        pltpu.make_async_copy(hidden_t_hbm, hidden_t_v, in_sems.at[0]),
        pltpu.make_async_copy(
            arrived_hbm.at[:, pl.ds(features, lanes)], pieces_v, in_sems.at[1]
        ),
    ]
    tiles = [
        pltpu.make_async_copy(
            arrived_hbm.at[:, pl.ds(part * tile, tile)], tiles_v.at[part], in_sems.at[2 + part]
        )
        for part in range(count)
    ]
    for copy in loads + tiles:
        copy.start()
    loads[1].wait()
    got = pieces_v[...].astype(jnp.float32)
    weights = (got[:, 0:1] + got[:, 1:2]) + got[:, 2:3]
    loads[0].wait()
    stores = []
    for part in range(count):
        tiles[part].wait()
        weighted = (weights * tiles_v[part].astype(jnp.float32)).astype(jnp.bfloat16)
        out_v[part] = jnp.dot(
            hidden_t_v[...], weighted, preferred_element_type=jnp.float32
        ).astype(jnp.bfloat16)
        store = pltpu.make_async_copy(
            out_v.at[part], partial_hbm.at[:, pl.ds(part * tile, tile)], out_sems.at[part]
        )
        store.start()
        stores.append(store)
    for store in stores:
        store.wait()


def weighted_partial(arrived, hidden_t, features):
    hidden_count, slots = hidden_t.shape
    lanes = arrived.shape[1] - features
    tile = 512 if features % 512 == 0 else features
    count = features // tile
    flops = 2 * slots * hidden_count * features
    moved = 2 * (arrived.size + hidden_t.size + hidden_count * features)
    anywhere = pl.BlockSpec(memory_space=pl.ANY)
    return pl.pallas_call(
        functools.partial(partial_kernel, tile=tile),
        out_shape=jax.ShapeDtypeStruct((hidden_count, features), jnp.bfloat16),
        in_specs=[anywhere, anywhere],
        out_specs=anywhere,
        scratch_shapes=[
            pltpu.VMEM((count, slots, tile), jnp.bfloat16),
            pltpu.VMEM((slots, lanes), jnp.bfloat16),
            pltpu.VMEM((hidden_count, slots), jnp.bfloat16),
            pltpu.VMEM((count, hidden_count, tile), jnp.bfloat16),
            pltpu.SemaphoreType.DMA((2 + count,)),
            pltpu.SemaphoreType.DMA((count,)),
        ],
        cost_estimate=pl.CostEstimate(flops=flops, bytes_accessed=moved, transcendentals=0),
    )(arrived, hidden_t)


def local(out_grad, combine_weight, routes, saved_gate, saved_up, w_down):
    experts = lax.axis_size("expert")
    tok_rows, route_count = routes.shape
    capacity = saved_gate.shape[3]
    hidden_count = saved_gate.shape[4]
    feature_count = out_grad.shape[1]
    slots = experts * capacity
    lanes = 128

    packed, position = pack_slots(routes.T, combine_weight.T, out_grad, experts, capacity)
    arrived = lax.all_to_all(
        packed.reshape(experts, capacity, feature_count + lanes),
        "expert",
        split_axis=0,
        concat_axis=0,
        tiled=True,
    ).reshape(slots, feature_count + lanes)
    rows = arrived[:, :feature_count]
    got = arrived[:, feature_count:feature_count + 3].astype(jnp.float32)
    weights = (got[:, 0] + got[:, 1]) + got[:, 2]

    gate_bf = saved_gate.reshape(-1, hidden_count)
    up_bf = saved_up.reshape(-1, hidden_count)
    hidden, hidden_t = hidden_pair(gate_bf, up_bf)
    partial_grad = weighted_partial(arrived, hidden_t, feature_count)
    summed = lax.psum_scatter(partial_grad, "dp", scatter_dimension=0, tiled=True)
    gate_pre = gate_bf.astype(jnp.float32)
    up_pre = up_bf.astype(jnp.float32)
    sigmoid_gate = jax.nn.sigmoid(gate_pre)
    grad_weight = summed.astype(jnp.float32)

    matrix = w_down[0]
    back = lax.dot_general(
        rows, matrix, (((1,), (1,)), ((), ())), preferred_element_type=jnp.float32
    )
    grad_hidden = weights[:, None] * back
    grad_gate = (
        grad_hidden * up_pre * sigmoid_gate * (1.0 + gate_pre * (1.0 - sigmoid_gate))
    ).astype(jnp.bfloat16)
    grad_up = (grad_hidden * gate_pre * sigmoid_gate).astype(jnp.bfloat16)
    slot_grad = jnp.sum(hidden.astype(jnp.float32) * back, axis=1)
    returned = lax.all_to_all(
        slot_grad.reshape(experts, capacity), "expert", split_axis=0, concat_axis=0, tiled=True
    )
    grad_combine = returned.reshape(-1)[position].T
    return (
        grad_weight[None],
        grad_gate.reshape(saved_gate.shape),
        grad_up.reshape(saved_up.shape),
        grad_combine,
    )


def solution(mesh):
    in_specs = (
        P(("expert", "dp"), None),
        P(("expert", "dp"), None),
        P(("expert", "dp"), None),
        P("expert", "dp", None, None, None),
        P("expert", "dp", None, None, None),
        P("expert", None, None),
    )
    out_specs = (
        P("expert", "dp", None),
        P("expert", "dp", None, None, None),
        P("expert", "dp", None, None, None),
        P(("expert", "dp"), None),
    )
    return jax.shard_map(local, mesh=mesh, in_specs=in_specs, out_specs=out_specs, check_vma=False)
```

```python
import functools

import jax
import jax.numpy as jnp
from jax import lax
from jax.sharding import PartitionSpec as P
from jax.experimental import pallas as pl
from jax.experimental.pallas import tpu as pltpu


def round_bf16(value):
    return lax.reduce_precision(value, exponent_bits=8, mantissa_bits=7)


def weight_pieces(weights):
    high = round_bf16(weights)
    rest = weights - high
    middle = round_bf16(rest)
    low = rest - middle
    return jnp.stack([high, middle, low], axis=-1).astype(jnp.bfloat16)


def front_kernel(routes_ref, weights_ref, rows_ref, packed_ref, position_ref, *, experts, capacity):
    route_count, tokens = routes_ref.shape
    slots, width = packed_ref.shape
    features = rows_ref.shape[1]
    padded = -(-experts // 8) * 8
    routes = routes_ref[...]
    expert_col = lax.broadcasted_iota(jnp.int32, (padded, tokens), 0)
    per_token = jnp.zeros((padded, tokens), jnp.float32)
    for k in range(route_count):
        per_token = per_token + jnp.where(routes[k:k + 1, :] == expert_col, 1.0, 0.0)
    earlier = jnp.where(
        lax.broadcasted_iota(jnp.int32, (tokens, tokens), 0)
        < lax.broadcasted_iota(jnp.int32, (tokens, tokens), 1), 1.0, 0.0
    ).astype(jnp.bfloat16)
    before = jnp.dot(per_token.astype(jnp.bfloat16), earlier, preferred_element_type=jnp.float32)
    slot_row = lax.broadcasted_iota(jnp.int32, (slots, tokens), 0)
    pick = jnp.zeros((slots, tokens), jnp.float32)
    weight = jnp.zeros((slots, 1), jnp.float32)
    for k in range(route_count):
        mine = routes[k:k + 1, :] == expert_col
        slot = jnp.sum(jnp.where(mine, before, 0.0), axis=0, keepdims=True).astype(jnp.int32)
        place = routes[k:k + 1, :] * capacity + slot
        position_ref[k:k + 1, :] = place
        chosen = slot_row == place
        pick = pick + jnp.where(chosen, 1.0, 0.0)
        weight = weight + jnp.sum(
            jnp.where(chosen, weights_ref[k:k + 1, :], 0.0), axis=1, keepdims=True
        )
    pick = pick.astype(jnp.bfloat16)
    tile = 512 if features % 512 == 0 else features
    for start in range(0, features, tile):
        packed_ref[:, start:start + tile] = jnp.dot(
            pick, rows_ref[:, start:start + tile], preferred_element_type=jnp.float32
        ).astype(jnp.bfloat16)
    high = weight.astype(jnp.bfloat16).astype(jnp.float32)
    rest = weight - high
    middle = rest.astype(jnp.bfloat16).astype(jnp.float32)
    low = rest - middle
    column = lax.broadcasted_iota(jnp.int32, (slots, width - features), 1)
    pieces = jnp.where(column == 0, high, jnp.where(column == 1, middle, jnp.where(column == 2, low, 0.0)))
    packed_ref[:, features:] = pieces.astype(jnp.bfloat16)


def pack_slots(routes_t, weights_t, rows, experts, capacity):
    route_count, tokens = routes_t.shape
    features = rows.shape[1]
    slots = experts * capacity
    vmem = pl.BlockSpec(memory_space=pltpu.VMEM)
    return pl.pallas_call(
        functools.partial(front_kernel, experts=experts, capacity=capacity),
        out_shape=(
            jax.ShapeDtypeStruct((slots, features + 128), jnp.bfloat16),
            jax.ShapeDtypeStruct((route_count, tokens), jnp.int32),
        ),
        in_specs=[vmem, vmem, vmem],
        out_specs=(vmem, vmem),
        cost_estimate=pl.CostEstimate(
            flops=2 * slots * tokens * features, bytes_accessed=2 * (rows.size + slots * features),
            transcendentals=0,
        ),
    )(routes_t, weights_t, rows)


def hidden_kernel(gate_ref, up_ref, hidden_ref, hidden_t_ref):
    gate = gate_ref[...].astype(jnp.float32)
    sigmoid_gate = 1.0 / (1.0 + jnp.exp(-gate))
    hidden = (gate * sigmoid_gate * up_ref[...].astype(jnp.float32)).astype(jnp.bfloat16)
    hidden_ref[...] = hidden
    hidden_t_ref[...] = jnp.transpose(hidden.astype(jnp.float32)).astype(jnp.bfloat16)


def hidden_pair(gate, up):
    slots, hidden_count = gate.shape
    vmem = pl.BlockSpec(memory_space=pltpu.VMEM)
    return pl.pallas_call(
        hidden_kernel,
        out_shape=(
            jax.ShapeDtypeStruct((slots, hidden_count), jnp.bfloat16),
            jax.ShapeDtypeStruct((hidden_count, slots), jnp.bfloat16),
        ),
        in_specs=[vmem, vmem],
        out_specs=(vmem, vmem),
        cost_estimate=pl.CostEstimate(
            flops=8 * gate.size, bytes_accessed=8 * gate.size, transcendentals=gate.size
        ),
    )(gate, up)


def partial_kernel(arrived_hbm, hidden_t_hbm, partial_hbm, tiles_v, pieces_v, hidden_t_v,
                   out_v, in_sems, out_sems, *, tile):
    count = tiles_v.shape[0]
    features = count * tile
    lanes = pieces_v.shape[1]
    loads = [
        pltpu.make_async_copy(hidden_t_hbm, hidden_t_v, in_sems.at[0]),
        pltpu.make_async_copy(
            arrived_hbm.at[:, pl.ds(features, lanes)], pieces_v, in_sems.at[1]
        ),
    ]
    tiles = [
        pltpu.make_async_copy(
            arrived_hbm.at[:, pl.ds(part * tile, tile)], tiles_v.at[part], in_sems.at[2 + part]
        )
        for part in range(count)
    ]
    for copy in loads + tiles:
        copy.start()
    loads[1].wait()
    got = pieces_v[...].astype(jnp.float32)
    weights = (got[:, 0:1] + got[:, 1:2]) + got[:, 2:3]
    loads[0].wait()
    stores = []
    for part in range(count):
        tiles[part].wait()
        weighted = (weights * tiles_v[part].astype(jnp.float32)).astype(jnp.bfloat16)
        out_v[part] = jnp.dot(
            hidden_t_v[...], weighted, preferred_element_type=jnp.float32
        ).astype(jnp.bfloat16)
        store = pltpu.make_async_copy(
            out_v.at[part], partial_hbm.at[:, pl.ds(part * tile, tile)], out_sems.at[part]
        )
        store.start()
        stores.append(store)
    for store in stores:
        store.wait()


def weighted_partial(arrived, hidden_t, features):
    hidden_count, slots = hidden_t.shape
    lanes = arrived.shape[1] - features
    tile = 1024 if features % 1024 == 0 else features
    count = features // tile
    flops = 2 * slots * hidden_count * features
    moved = 2 * (arrived.size + hidden_t.size + hidden_count * features)
    anywhere = pl.BlockSpec(memory_space=pl.ANY)
    return pl.pallas_call(
        functools.partial(partial_kernel, tile=tile),
        out_shape=jax.ShapeDtypeStruct((hidden_count, features), jnp.bfloat16),
        in_specs=[anywhere, anywhere],
        out_specs=anywhere,
        scratch_shapes=[
            pltpu.VMEM((count, slots, tile), jnp.bfloat16),
            pltpu.VMEM((slots, lanes), jnp.bfloat16),
            pltpu.VMEM((hidden_count, slots), jnp.bfloat16),
            pltpu.VMEM((count, hidden_count, tile), jnp.bfloat16),
            pltpu.SemaphoreType.DMA((2 + count,)),
            pltpu.SemaphoreType.DMA((count,)),
        ],
        cost_estimate=pl.CostEstimate(flops=flops, bytes_accessed=moved, transcendentals=0),
    )(arrived, hidden_t)


def local(out_grad, combine_weight, routes, saved_gate, saved_up, w_down):
    experts = lax.axis_size("expert")
    tok_rows, route_count = routes.shape
    capacity = saved_gate.shape[3]
    hidden_count = saved_gate.shape[4]
    feature_count = out_grad.shape[1]
    slots = experts * capacity
    lanes = 128

    packed, position = pack_slots(routes.T, combine_weight.T, out_grad, experts, capacity)
    arrived = lax.all_to_all(
        packed.reshape(experts, capacity, feature_count + lanes),
        "expert",
        split_axis=0,
        concat_axis=0,
        tiled=True,
    ).reshape(slots, feature_count + lanes)
    rows = arrived[:, :feature_count]
    got = arrived[:, feature_count:feature_count + 3].astype(jnp.float32)
    weights = (got[:, 0] + got[:, 1]) + got[:, 2]

    gate_bf = saved_gate.reshape(-1, hidden_count)
    up_bf = saved_up.reshape(-1, hidden_count)
    hidden, hidden_t = hidden_pair(gate_bf, up_bf)
    partial_grad = weighted_partial(arrived, hidden_t, feature_count)
    summed = lax.psum_scatter(partial_grad, "dp", scatter_dimension=0, tiled=True)
    gate_pre = gate_bf.astype(jnp.float32)
    up_pre = up_bf.astype(jnp.float32)
    sigmoid_gate = jax.nn.sigmoid(gate_pre)
    grad_weight = summed.astype(jnp.float32)

    matrix = w_down[0]
    back = lax.dot_general(
        rows, matrix, (((1,), (1,)), ((), ())), preferred_element_type=jnp.float32
    )
    grad_hidden = weights[:, None] * back
    grad_gate = (
        grad_hidden * up_pre * sigmoid_gate * (1.0 + gate_pre * (1.0 - sigmoid_gate))
    ).astype(jnp.bfloat16)
    grad_up = (grad_hidden * gate_pre * sigmoid_gate).astype(jnp.bfloat16)
    slot_grad = jnp.sum(hidden.astype(jnp.float32) * back, axis=1)
    returned = lax.all_to_all(
        slot_grad.reshape(experts, capacity), "expert", split_axis=0, concat_axis=0, tiled=True
    )
    grad_combine = returned.reshape(-1)[position].T
    return (
        grad_weight[None],
        grad_gate.reshape(saved_gate.shape),
        grad_up.reshape(saved_up.shape),
        grad_combine,
    )


def solution(mesh):
    in_specs = (
        P(("expert", "dp"), None),
        P(("expert", "dp"), None),
        P(("expert", "dp"), None),
        P("expert", "dp", None, None, None),
        P("expert", "dp", None, None, None),
        P("expert", None, None),
    )
    out_specs = (
        P("expert", "dp", None),
        P("expert", "dp", None, None, None),
        P("expert", "dp", None, None, None),
        P(("expert", "dp"), None),
    )
    return jax.shard_map(local, mesh=mesh, in_specs=in_specs, out_specs=out_specs, check_vma=False)
```

```python
import functools

import jax
import jax.numpy as jnp
from jax import lax
from jax.sharding import PartitionSpec as P
from jax.experimental import pallas as pl
from jax.experimental.pallas import tpu as pltpu


def round_bf16(value):
    return lax.reduce_precision(value, exponent_bits=8, mantissa_bits=7)


def weight_pieces(weights):
    high = round_bf16(weights)
    rest = weights - high
    middle = round_bf16(rest)
    low = rest - middle
    return jnp.stack([high, middle, low], axis=-1).astype(jnp.bfloat16)


def front_kernel(routes_ref, weights_ref, rows_ref, packed_ref, position_ref, *, experts, capacity):
    route_count, tokens = routes_ref.shape
    slots, width = packed_ref.shape
    features = rows_ref.shape[1]
    padded = -(-experts // 8) * 8
    routes = routes_ref[...]
    expert_col = lax.broadcasted_iota(jnp.int32, (padded, tokens), 0)
    per_token = jnp.zeros((padded, tokens), jnp.float32)
    for k in range(route_count):
        per_token = per_token + jnp.where(routes[k:k + 1, :] == expert_col, 1.0, 0.0)
    earlier = jnp.where(
        lax.broadcasted_iota(jnp.int32, (tokens, tokens), 0)
        < lax.broadcasted_iota(jnp.int32, (tokens, tokens), 1), 1.0, 0.0
    ).astype(jnp.bfloat16)
    before = jnp.dot(per_token.astype(jnp.bfloat16), earlier, preferred_element_type=jnp.float32)
    slot_row = lax.broadcasted_iota(jnp.int32, (slots, tokens), 0)
    pick = jnp.zeros((slots, tokens), jnp.float32)
    weight = jnp.zeros((slots, 1), jnp.float32)
    for k in range(route_count):
        mine = routes[k:k + 1, :] == expert_col
        slot = jnp.sum(jnp.where(mine, before, 0.0), axis=0, keepdims=True).astype(jnp.int32)
        place = routes[k:k + 1, :] * capacity + slot
        position_ref[k:k + 1, :] = place
        chosen = slot_row == place
        pick = pick + jnp.where(chosen, 1.0, 0.0)
        weight = weight + jnp.sum(
            jnp.where(chosen, weights_ref[k:k + 1, :], 0.0), axis=1, keepdims=True
        )
    pick = pick.astype(jnp.bfloat16)
    tile = 512 if features % 512 == 0 else features
    for start in range(0, features, tile):
        packed_ref[:, start:start + tile] = jnp.dot(
            pick, rows_ref[:, start:start + tile], preferred_element_type=jnp.float32
        ).astype(jnp.bfloat16)
    high = weight.astype(jnp.bfloat16).astype(jnp.float32)
    rest = weight - high
    middle = rest.astype(jnp.bfloat16).astype(jnp.float32)
    low = rest - middle
    column = lax.broadcasted_iota(jnp.int32, (slots, width - features), 1)
    pieces = jnp.where(column == 0, high, jnp.where(column == 1, middle, jnp.where(column == 2, low, 0.0)))
    packed_ref[:, features:] = pieces.astype(jnp.bfloat16)


def pack_slots(routes_t, weights_t, rows, experts, capacity):
    route_count, tokens = routes_t.shape
    features = rows.shape[1]
    slots = experts * capacity
    vmem = pl.BlockSpec(memory_space=pltpu.VMEM)
    return pl.pallas_call(
        functools.partial(front_kernel, experts=experts, capacity=capacity),
        out_shape=(
            jax.ShapeDtypeStruct((slots, features + 128), jnp.bfloat16),
            jax.ShapeDtypeStruct((route_count, tokens), jnp.int32),
        ),
        in_specs=[vmem, vmem, vmem],
        out_specs=(vmem, vmem),
        cost_estimate=pl.CostEstimate(
            flops=2 * slots * tokens * features, bytes_accessed=2 * (rows.size + slots * features),
            transcendentals=0,
        ),
    )(routes_t, weights_t, rows)


def hidden_kernel(gate_ref, up_ref, hidden_ref, hidden_t_ref):
    gate = gate_ref[...].astype(jnp.float32)
    sigmoid_gate = 1.0 / (1.0 + jnp.exp(-gate))
    hidden = (gate * sigmoid_gate * up_ref[...].astype(jnp.float32)).astype(jnp.bfloat16)
    hidden_ref[...] = hidden
    hidden_t_ref[...] = jnp.transpose(hidden.astype(jnp.float32)).astype(jnp.bfloat16)


def hidden_pair(gate, up):
    slots, hidden_count = gate.shape
    vmem = pl.BlockSpec(memory_space=pltpu.VMEM)
    return pl.pallas_call(
        hidden_kernel,
        out_shape=(
            jax.ShapeDtypeStruct((slots, hidden_count), jnp.bfloat16),
            jax.ShapeDtypeStruct((hidden_count, slots), jnp.bfloat16),
        ),
        in_specs=[vmem, vmem],
        out_specs=(vmem, vmem),
        cost_estimate=pl.CostEstimate(
            flops=8 * gate.size, bytes_accessed=8 * gate.size, transcendentals=gate.size
        ),
    )(gate, up)


def partial_kernel(arrived_hbm, hidden_t_hbm, partial_hbm, tiles_v, pieces_v, hidden_t_v,
                   out_v, in_sems, out_sems, *, tile):
    count = tiles_v.shape[0]
    features = count * tile
    lanes = pieces_v.shape[1]
    loads = [
        pltpu.make_async_copy(hidden_t_hbm, hidden_t_v, in_sems.at[0]),
        pltpu.make_async_copy(
            arrived_hbm.at[:, pl.ds(features, lanes)], pieces_v, in_sems.at[1]
        ),
    ]
    tiles = [
        pltpu.make_async_copy(
            arrived_hbm.at[:, pl.ds(part * tile, tile)], tiles_v.at[part], in_sems.at[2 + part]
        )
        for part in range(count)
    ]
    for copy in loads + tiles:
        copy.start()
    loads[1].wait()
    got = pieces_v[...].astype(jnp.float32)
    weights = (got[:, 0:1] + got[:, 1:2]) + got[:, 2:3]
    loads[0].wait()
    stores = []
    for part in range(count):
        tiles[part].wait()
        weighted = (weights * tiles_v[part].astype(jnp.float32)).astype(jnp.bfloat16)
        out_v[part] = jnp.dot(
            hidden_t_v[...], weighted, preferred_element_type=jnp.float32
        ).astype(jnp.bfloat16)
        store = pltpu.make_async_copy(
            out_v.at[part], partial_hbm.at[:, pl.ds(part * tile, tile)], out_sems.at[part]
        )
        store.start()
        stores.append(store)
    for store in stores:
        store.wait()


def weighted_partial(arrived, hidden_t, features):
    hidden_count, slots = hidden_t.shape
    lanes = arrived.shape[1] - features
    tile = 512 if features % 512 == 0 else features
    count = features // tile
    flops = 2 * slots * hidden_count * features
    moved = 2 * (arrived.size + hidden_t.size + hidden_count * features)
    anywhere = pl.BlockSpec(memory_space=pl.ANY)
    return pl.pallas_call(
        functools.partial(partial_kernel, tile=tile),
        out_shape=jax.ShapeDtypeStruct((hidden_count, features), jnp.bfloat16),
        in_specs=[anywhere, anywhere],
        out_specs=anywhere,
        scratch_shapes=[
            pltpu.VMEM((count, slots, tile), jnp.bfloat16),
            pltpu.VMEM((slots, lanes), jnp.bfloat16),
            pltpu.VMEM((hidden_count, slots), jnp.bfloat16),
            pltpu.VMEM((count, hidden_count, tile), jnp.bfloat16),
            pltpu.SemaphoreType.DMA((2 + count,)),
            pltpu.SemaphoreType.DMA((count,)),
        ],
        cost_estimate=pl.CostEstimate(flops=flops, bytes_accessed=moved, transcendentals=0),
    )(arrived, hidden_t)


def widen_kernel(narrow_ref, wide_ref):
    wide_ref[...] = narrow_ref[...].astype(jnp.float32)


def widen(narrow):
    vmem = pl.BlockSpec(memory_space=pltpu.VMEM)
    return pl.pallas_call(
        widen_kernel,
        out_shape=jax.ShapeDtypeStruct(narrow.shape, jnp.float32),
        in_specs=[vmem],
        out_specs=vmem,
        cost_estimate=pl.CostEstimate(
            flops=narrow.size, bytes_accessed=6 * narrow.size, transcendentals=0
        ),
    )(narrow)


def local(out_grad, combine_weight, routes, saved_gate, saved_up, w_down):
    experts = lax.axis_size("expert")
    tok_rows, route_count = routes.shape
    capacity = saved_gate.shape[3]
    hidden_count = saved_gate.shape[4]
    feature_count = out_grad.shape[1]
    slots = experts * capacity
    lanes = 128

    packed, position = pack_slots(routes.T, combine_weight.T, out_grad, experts, capacity)
    arrived = lax.all_to_all(
        packed.reshape(experts, capacity, feature_count + lanes),
        "expert",
        split_axis=0,
        concat_axis=0,
        tiled=True,
    ).reshape(slots, feature_count + lanes)
    rows = arrived[:, :feature_count]
    got = arrived[:, feature_count:feature_count + 3].astype(jnp.float32)
    weights = (got[:, 0] + got[:, 1]) + got[:, 2]

    gate_bf = saved_gate.reshape(-1, hidden_count)
    up_bf = saved_up.reshape(-1, hidden_count)
    hidden, hidden_t = hidden_pair(gate_bf, up_bf)
    partial_grad = weighted_partial(arrived, hidden_t, feature_count)
    summed = lax.psum_scatter(partial_grad, "dp", scatter_dimension=0, tiled=True)
    gate_pre = gate_bf.astype(jnp.float32)
    up_pre = up_bf.astype(jnp.float32)
    sigmoid_gate = jax.nn.sigmoid(gate_pre)
    grad_weight = widen(summed)

    matrix = w_down[0]
    back = lax.dot_general(
        rows, matrix, (((1,), (1,)), ((), ())), preferred_element_type=jnp.float32
    )
    grad_hidden = weights[:, None] * back
    grad_gate = (
        grad_hidden * up_pre * sigmoid_gate * (1.0 + gate_pre * (1.0 - sigmoid_gate))
    ).astype(jnp.bfloat16)
    grad_up = (grad_hidden * gate_pre * sigmoid_gate).astype(jnp.bfloat16)
    slot_grad = jnp.sum(hidden.astype(jnp.float32) * back, axis=1)
    returned = lax.all_to_all(
        slot_grad.reshape(experts, capacity), "expert", split_axis=0, concat_axis=0, tiled=True
    )
    grad_combine = returned.reshape(-1)[position].T
    return (
        grad_weight[None],
        grad_gate.reshape(saved_gate.shape),
        grad_up.reshape(saved_up.shape),
        grad_combine,
    )


def solution(mesh):
    in_specs = (
        P(("expert", "dp"), None),
        P(("expert", "dp"), None),
        P(("expert", "dp"), None),
        P("expert", "dp", None, None, None),
        P("expert", "dp", None, None, None),
        P("expert", None, None),
    )
    out_specs = (
        P("expert", "dp", None),
        P("expert", "dp", None, None, None),
        P("expert", "dp", None, None, None),
        P(("expert", "dp"), None),
    )
    return jax.shard_map(local, mesh=mesh, in_specs=in_specs, out_specs=out_specs, check_vma=False)
```
